128 devices in a mesh: dp: 4 (over x), head: 8 (over y, core), blk: 4 (over z).
Axes of the slice: x: 4, y: 4, z: 4, core: 2. Of those that a mesh axis runs over, the one named last changes fastest.
Arguments:
- query: bfloat16 [65536, 2048], P(('dp', 'head', 'blk')), parts along dimension 0, may hold values from -7 to 7
- key: bfloat16 [65536, 2048], P(('dp', 'head', 'blk')), parts along dimension 0, may hold values from -7 to 7
- value: bfloat16 [65536, 2048], P(('dp', 'head', 'blk')), parts along dimension 0, may hold values from -30 to 30
- dout: bfloat16 [65536, 2048], P(('dp', 'head', 'blk')), parts along dimension 0, may hold values from -30 to 30
- rand: int32 [1024, 3], P('dp'), parts along dimension 0, may hold values from 0 to 255, as said below
Outputs:
- out: bfloat16 [65536, 2048], P(('dp', 'head', 'blk')), parts along dimension 0
- dq: bfloat16 [65536, 2048], P(('dp', 'head', 'blk')), parts along dimension 0
- dk: bfloat16 [65536, 2048], P(('dp', 'head', 'blk')), parts along dimension 0
- dv: bfloat16 [65536, 2048], P(('dp', 'head', 'blk')), parts along dimension 0
The draws below stay inside these ranges and needn't reach their ends.
There are 4 independent parts, one for each index of `dp`. The reference program is written for one: setup_inputs(seed, part) draws one part's arguments, and reference() takes and returns one part's arrays. A program takes and returns all parts, laid end to end along the dimension named above; each array names one. Nothing has to cross between parts.
Inputs may be any that keep to these rules, and one draw needn't show every extreme that they name: `rand`: for each group of 8 consecutive query blocks (the rows of one device), at most 1 of its 24 random blocks fall in any one group of 8 consecutive blocks.
All inputs are finite; a program needn't handle non-finite values.
Results may differ from the reference program's by a relative error of at most 0.023.
Values may be sent and summed in bfloat16 or wider, within the bound.
No kernel may reach another device: no remote copies, remote signals or barrier semaphores. Data moves between devices by JAX's collectives and lax.ppermute only.
A program may use at most 448 MiB of HBM per device.

```python
import math
import jax
import jax.numpy as jnp
from jax import lax

H = 16
HD = 128
BS = 64
R = 3
SEQDEV = 32
L = 16384
NBD = 8
NB = 256
CAP = 1


def draw_query(key, part):
    own = jax.random.fold_in(key, 21)
    field = jnp.clip(jax.random.normal(own, (L, H * HD), jnp.float32), -4.0, 4.0)
    return field.astype(jnp.bfloat16)


def draw_key(key, part):
    own = jax.random.fold_in(key, 22)
    field = jnp.clip(jax.random.normal(own, (L, H * HD), jnp.float32), -4.0, 4.0)
    return field.astype(jnp.bfloat16)


def draw_rand(key, part):
    streams = jax.random.split(jax.random.fold_in(key, 31), SEQDEV)
    perms = jax.vmap(lambda stream: jax.random.permutation(stream, SEQDEV * CAP))(streams)[:, :NBD * R]
    owner = perms // CAP
    local = jax.random.randint(jax.random.fold_in(key, 32), (SEQDEV, NBD * R), 0, NBD)
    return (owner * NBD + local).reshape(NB, R).astype(jnp.int32)


def steps_of(stream_key, extent, cuts, low, high):
    loudness, own = 1.0, jax.random.fold_in(stream_key, 6)
    for axis_at, parts in cuts:
        heights = jnp.exp(jax.random.uniform(jax.random.fold_in(own, axis_at), (parts,), jnp.float32, low / len(cuts), high / len(cuts)))
        loudness = loudness * jnp.repeat(heights, extent[axis_at] // parts).reshape([-1 if axis == axis_at else 1 for axis in range(len(extent))])
    return loudness


def noise(stream_key, dims, deviation, most, cuts=(), kind=jnp.bfloat16):
    factor_of = steps_of(stream_key, dims, cuts, -0.22, 0.18) if cuts else 1.0
    drawn = jax.random.normal(stream_key, dims, jnp.float32) * deviation * factor_of
    return jnp.minimum(jnp.maximum(drawn, -most), most).astype(kind)


def setup_inputs(seed: int = 0, part: int = 0) -> dict:
    key_list = jax.random.split(jax.random.key(seed), 6)
    own_keys = jax.random.split(jax.random.fold_in(key_list[5], part), 6)
    return {
        "query": draw_query(jax.random.fold_in(jax.random.fold_in(key_list[5], part), 71), part),
        "key": draw_key(jax.random.fold_in(jax.random.fold_in(key_list[5], part), 71), part),
        "value": noise(own_keys[2], (L, H * HD), 5.0, 30.0, ((0, 32),)),
        "dout": noise(own_keys[3], (L, H * HD), 5.0, 30.0, ((0, 32),)),
        "rand": draw_rand(jax.random.fold_in(jax.random.fold_in(key_list[5], part), 71), part),
    }


NEG = -1e+30

def reference(query, key, value, dout, rand):
    scale = 1.0 / math.sqrt(HD)
    q4 = query.reshape(NB, BS, H, HD)
    k4 = key.reshape(NB, BS, H, HD)
    v4 = value.reshape(NB, BS, H, HD)
    d4 = dout.reshape(NB, BS, H, HD)
    is_random = jnp.arange(5 + R) >= 5

    def step(carry, index):
        grad_key, grad_value = carry
        fixed = jnp.stack([index - 1, index, index + 1, index * 0, index * 0 + 1])
        listed = jnp.concatenate([fixed.astype(jnp.int32), rand[index].astype(jnp.int32)])
        valid = jnp.concatenate([jnp.stack([index > 0, index >= 0, index < NB - 1, index >= 0, index >= 0]), jnp.ones((R,), bool)])
        clipped = jnp.clip(listed, 0, NB - 1).astype(jnp.int32)
        keys = jnp.take(k4, clipped, axis=0).astype(jnp.float32)
        values = jnp.take(v4, clipped, axis=0).astype(jnp.float32)
        rows = q4[index].astype(jnp.float32)
        grads = d4[index].astype(jnp.float32)
        scores = jnp.einsum('qhd,gkhd->hqgk', rows, keys) * scale
        scores = jnp.where(valid[None, None, :, None], scores, NEG)
        top = lax.optimization_barrier(jnp.max(scores, axis=(2, 3), keepdims=True))
        expo = jnp.exp(scores - top)
        probs = expo / lax.optimization_barrier(jnp.sum(expo, axis=(2, 3), keepdims=True))
        probs_b = lax.optimization_barrier(probs.astype(jnp.bfloat16)).astype(jnp.float32)
        result = jnp.einsum('hqgk,gkhd->qhd', probs_b, values).astype(jnp.bfloat16)
        delta = jnp.einsum('qhd,qhd->hq', grads, result.astype(jnp.float32))
        dprob = jnp.einsum('qhd,gkhd->hqgk', grads, values)
        dscore = probs * (dprob - delta[:, :, None, None])
        dscore_b = lax.optimization_barrier(dscore.astype(jnp.bfloat16)).astype(jnp.float32)
        grad_query = (jnp.einsum('hqgk,gkhd->qhd', dscore_b, keys) * scale).astype(jnp.bfloat16)
        key_terms = jnp.einsum('hqgk,qhd->gkhd', dscore_b, rows) * scale
        value_terms = jnp.einsum('hqgk,qhd->gkhd', probs_b, grads)
        key_round = lax.optimization_barrier(key_terms.astype(jnp.bfloat16)).astype(jnp.float32)
        value_round = lax.optimization_barrier(value_terms.astype(jnp.bfloat16)).astype(jnp.float32)
        picked = is_random[:, None, None, None]
        key_terms = jnp.where(picked, key_round, key_terms)
        value_terms = jnp.where(picked, value_round, value_terms)
        grad_key = grad_key.at[clipped].add(key_terms)
        grad_value = grad_value.at[clipped].add(value_terms)
        return ((grad_key, grad_value), (result, grad_query))
    start = (jnp.zeros((NB, BS, H, HD), jnp.float32), jnp.zeros((NB, BS, H, HD), jnp.float32))
    (grad_key, grad_value), (result, grad_query) = lax.scan(step, start, jnp.arange(NB, dtype=jnp.int32))
    out = result.reshape(L, H * HD)
    dq = grad_query.reshape(L, H * HD)
    dk = grad_key.astype(jnp.bfloat16).reshape(L, H * HD)
    dv = grad_value.astype(jnp.bfloat16).reshape(L, H * HD)
    return (out, dq, dk, dv)
```

```python
import math

import jax
import jax.numpy as jnp
from jax import lax
from jax.experimental import pallas as pl
from jax.experimental.pallas import tpu as pltpu
from jax.sharding import PartitionSpec as P

HD = 128
BS = 64
R = 3


NEG = -1e30
INTERPRET = False


def extended(block, sides, width):
    for axis, dim in sides:
        count = lax.axis_size(axis)
        forward = [(i, i + 1) for i in range(count - 1)]
        backward = [(target, source) for source, target in forward]
        low = lax.ppermute(
            lax.slice_in_dim(block, block.shape[dim] - width, None, axis=dim), axis, forward
        )
        high = lax.ppermute(lax.slice_in_dim(block, 0, width, axis=dim), axis, backward)
        block = jnp.concatenate([low, block, high], axis=dim)
    return block


def from_root(value, axis, source):
    kept = jnp.where(lax.axis_index(axis) == source, value, 0).astype(value.dtype)
    return lax.psum(kept, axis)


def attention_kernel(
    slots_ref, q_ref, do_ref, mask_ref,
    kw0, kw1, kw2, vw0, vw1, vw2, kg, vg, kr0, kr1, kr2, vr0, vr1, vr2,
    out_ref, dq_ref, wk_ref, wv_ref, gk_ref, gv_ref, rk_ref, rv_ref,
):
    pf = jnp.float32
    scale = 1.0 / math.sqrt(HD)
    q = q_ref[...]
    do = do_ref[...]
    k = jnp.concatenate([kw0[...], kw1[...], kw2[...], kg[...], kr0[0], kr1[0], kr2[0]], axis=0)
    v = jnp.concatenate([vw0[...], vw1[...], vw2[...], vg[...], vr0[0], vr1[0], vr2[0]], axis=0)
    nt = (((1,), (1,)), ((), ()))
    s = lax.dot_general(q, k, nt, preferred_element_type=pf) * scale
    s = jnp.where(mask_ref[0] > 0, s, NEG)
    top = jnp.max(s, axis=1, keepdims=True)
    e = jnp.exp(s - top)
    p = e / jnp.sum(e, axis=1, keepdims=True)
    pb = p.astype(jnp.bfloat16)
    ob = jnp.dot(pb, v, preferred_element_type=pf).astype(jnp.bfloat16)
    out_ref[...] = ob
    delta = jnp.sum(do.astype(pf) * ob.astype(pf), axis=1, keepdims=True)
    dp = lax.dot_general(do, v, nt, preferred_element_type=pf)
    ds = p * (dp - delta)
    dsb = ds.astype(jnp.bfloat16)
    dq_ref[...] = (jnp.dot(dsb, k, preferred_element_type=pf) * scale).astype(jnp.bfloat16)
    kt = jnp.dot(ds.T.astype(jnp.bfloat16), q, preferred_element_type=pf) * scale
    vt = jnp.dot(p.T.astype(jnp.bfloat16), do, preferred_element_type=pf)
    w = 3 * BS
    g = 5 * BS
    wk_ref[0] = kt[:w]
    wv_ref[0] = vt[:w]
    gk_ref[0] = kt[w:g]
    gv_ref[0] = vt[w:g]
    rk_ref[0] = kt[g:].astype(jnp.bfloat16)
    rv_ref[0] = vt[g:].astype(jnp.bfloat16)


def attention(query, dout, mask, padded, glob, fetched, slots):
    rows, width = query.shape
    heads = width // HD
    nbd = rows // BS
    span = (5 + R) * BS

    def tile(j, col):
        return pl.BlockSpec((BS, HD), lambda n, h, s: (n + j, h + col))

    def rand_tile(j, col):
        return pl.BlockSpec((1, BS, HD), lambda n, h, s: (s[n * R + j], 0, h + col))

    row_spec = pl.BlockSpec((BS, HD), lambda n, h, s: (n, h))
    in_specs = (
        [row_spec, row_spec, pl.BlockSpec((1, 1, span), lambda n, h, s: (n, 0, 0))]
        + [tile(j, 0) for j in range(3)]
        + [tile(j, heads) for j in range(3)]
        + [
            pl.BlockSpec((2 * BS, HD), lambda n, h, s: (0, h)),
            pl.BlockSpec((2 * BS, HD), lambda n, h, s: (0, h + heads)),
        ]
        + [rand_tile(j, 0) for j in range(R)]
        + [rand_tile(j, heads) for j in range(R)]
    )

    def term_spec(size):
        return pl.BlockSpec((1, size, HD), lambda n, h, s: (n, 0, h))

    out_specs = [
        row_spec,
        row_spec,
        term_spec(3 * BS),
        term_spec(3 * BS),
        term_spec(2 * BS),
        term_spec(2 * BS),
        term_spec(R * BS),
        term_spec(R * BS),
    ]
    out_shape = [
        jax.ShapeDtypeStruct((rows, width), jnp.bfloat16),
        jax.ShapeDtypeStruct((rows, width), jnp.bfloat16),
        jax.ShapeDtypeStruct((nbd, 3 * BS, width), jnp.float32),
        jax.ShapeDtypeStruct((nbd, 3 * BS, width), jnp.float32),
        jax.ShapeDtypeStruct((nbd, 2 * BS, width), jnp.float32),
        jax.ShapeDtypeStruct((nbd, 2 * BS, width), jnp.float32),
        jax.ShapeDtypeStruct((nbd, R * BS, width), jnp.bfloat16),
        jax.ShapeDtypeStruct((nbd, R * BS, width), jnp.bfloat16),
    ]
    grid_spec = pltpu.PrefetchScalarGridSpec(
        num_scalar_prefetch=1,
        grid=(nbd, heads),
        in_specs=in_specs,
        out_specs=out_specs,
    )
    args = [query, dout, mask] + [padded] * 6 + [glob] * 2 + [fetched] * (2 * R)
    return pl.pallas_call(
        attention_kernel,
        grid_spec=grid_spec,
        out_shape=out_shape,
        interpret=INTERPRET,
    )(slots, *args)


def overlap(terms, nbd):
    width = terms.shape[-1]
    w4 = terms.reshape(nbd, 3, BS, width)
    return (
        jnp.pad(w4[:, 0], ((0, 2), (0, 0), (0, 0)))
        + jnp.pad(w4[:, 1], ((1, 1), (0, 0), (0, 0)))
        + jnp.pad(w4[:, 2], ((2, 0), (0, 0), (0, 0)))
    )


def body(query, key, value, dout, rand):
    rows, width = query.shape
    ndev = lax.axis_size(("head", "blk"))
    me = lax.axis_index(("head", "blk"))
    nbd = rows // BS
    total = nbd * ndev
    cap = (R * nbd + ndev - 1) // ndev
    pf = jnp.float32
    span = (5 + R) * BS
    pair = jnp.concatenate([key, value], axis=1)
    padded = extended(pair, ((("head", "blk"), 0),), BS)
    glob = from_root(pair[: 2 * BS], ("head", "blk"), 0)
    flat = rand.reshape(ndev, nbd * R)
    owner = flat // nbd
    local = flat - owner * nbd
    hit = owner == me
    order = jnp.cumsum(hit.astype(jnp.int32), axis=1) - 1
    slot_ids = jnp.arange(cap, dtype=jnp.int32)
    chosen = hit[:, None, :] & (order[:, None, :] == slot_ids[None, :, None])
    block_id = jnp.sum(jnp.where(chosen, local[:, None, :], 0), axis=2).reshape(-1)
    filled = jnp.any(chosen, axis=2).reshape(-1)
    tiles = pair.reshape(nbd, BS, 2 * width)
    outgoing = jnp.where(
        filled[:, None, None], jnp.take(tiles, block_id, axis=0), jnp.zeros((), pair.dtype)
    )
    fetched = lax.all_to_all(outgoing, ("head", "blk"), split_axis=0, concat_axis=0, tiled=True)
    mine = lax.dynamic_slice_in_dim(rand, me * nbd, nbd, 0).reshape(-1)
    mine_owner = mine // nbd
    count = mine.shape[0]
    earlier = jnp.arange(count)[:, None] > jnp.arange(count)[None, :]
    same = mine_owner[:, None] == mine_owner[None, :]
    mine_rank = jnp.sum(earlier & same, axis=1)
    mine_slot = (mine_owner * cap + mine_rank).astype(jnp.int32)
    first = me * nbd + jnp.arange(nbd, dtype=jnp.int32)
    always = first >= 0
    valid = jnp.concatenate(
        [
            jnp.stack([first > 0, always, first < total - 1, always, always], axis=1),
            jnp.ones((nbd, R), bool),
        ],
        axis=1,
    )
    mask = jnp.repeat(valid, BS, axis=1).astype(pf).reshape(nbd, 1, span)
    out, dq, wk, wv, gk, gv, rk, rv = attention(query, dout, mask, padded, glob, fetched, mine_slot)
    sk = overlap(wk, nbd)
    sv = overlap(wv, nbd)
    rims = jnp.concatenate(
        [
            jnp.concatenate([sk[0], sv[0]], axis=-1),
            jnp.concatenate([sk[nbd + 1], sv[nbd + 1]], axis=-1),
        ],
        axis=0,
    )
    arrived = extended(rims.astype(jnp.bfloat16), ((("head", "blk"), 0),), BS).astype(pf)
    own = jnp.concatenate([sk[1 : nbd + 1], sv[1 : nbd + 1]], axis=-1)
    own = own.at[0].add(arrived[:BS]).at[nbd - 1].add(arrived[3 * BS :])
    glob_grad = jnp.concatenate([jnp.sum(gk, axis=0), jnp.sum(gv, axis=0)], axis=-1).reshape(
        2, BS, 2 * width
    )
    glob_total = lax.psum(glob_grad.astype(jnp.bfloat16), ("head", "blk")).astype(pf)
    own = own.at[:2].add(jnp.where(me == 0, glob_total, 0.0))
    rand_grad = jnp.concatenate([rk, rv], axis=-1).reshape(nbd * R, BS, 2 * width)
    returning = jnp.zeros((ndev * cap, BS, 2 * width), jnp.bfloat16).at[mine_slot].set(rand_grad)
    back = lax.all_to_all(returning, ("head", "blk"), split_axis=0, concat_axis=0, tiled=True)
    onehot = (
        (block_id[None, :] == jnp.arange(nbd, dtype=jnp.int32)[:, None]) & filled[None, :]
    ).astype(jnp.bfloat16)
    own = own + jnp.dot(
        onehot, back.reshape(ndev * cap, BS * 2 * width), preferred_element_type=pf
    ).reshape(nbd, BS, 2 * width)
    dk = own[..., :width].astype(jnp.bfloat16).reshape(rows, width)
    dv = own[..., width:].astype(jnp.bfloat16).reshape(rows, width)
    return (out, dq, dk, dv)


def solution(mesh):
    placed = (
        P(("dp", "head", "blk"), None),
        P(("dp", "head", "blk"), None),
        P(("dp", "head", "blk"), None),
        P(("dp", "head", "blk"), None),
        P("dp", None),
    )
    return jax.shard_map(
        body,
        mesh=mesh,
        in_specs=placed,
        out_specs=(
            P(("dp", "head", "blk"), None),
            P(("dp", "head", "blk"), None),
            P(("dp", "head", "blk"), None),
            P(("dp", "head", "blk"), None),
        ),
        check_vma=False,
    )
```

```python
import math

import jax
import jax.numpy as jnp
from jax import lax
from jax.experimental import pallas as pl
from jax.experimental.pallas import tpu as pltpu
from jax.sharding import PartitionSpec as P

HD = 128
BS = 64
R = 3


NEG = -1e30
INTERPRET = False


def extended(block, sides, width):
    for axis, dim in sides:
        count = lax.axis_size(axis)
        forward = [(i, i + 1) for i in range(count - 1)]
        backward = [(target, source) for source, target in forward]
        low = lax.ppermute(
            lax.slice_in_dim(block, block.shape[dim] - width, None, axis=dim), axis, forward
        )
        high = lax.ppermute(lax.slice_in_dim(block, 0, width, axis=dim), axis, backward)
        block = jnp.concatenate([low, block, high], axis=dim)
    return block


def from_root(value, axis, source):
    kept = jnp.where(lax.axis_index(axis) == source, value, 0).astype(value.dtype)
    return lax.psum(kept, axis)


def scores_kernel(
    slots_ref, q_ref, do_ref, mask_ref,
    kw0, kw1, kw2, vw0, vw1, vw2, kg, vg, kr0, kr1, kr2, vr0, vr1, vr2,
    out_ref, dq_ref, rk_ref, rv_ref, pb_ref, dsb_ref,
):
    pf = jnp.float32
    scale = 1.0 / math.sqrt(HD)
    q = q_ref[...]
    do = do_ref[...]
    k = jnp.concatenate([kw0[...], kw1[...], kw2[...], kg[...], kr0[0], kr1[0], kr2[0]], axis=0)
    v = jnp.concatenate([vw0[...], vw1[...], vw2[...], vg[...], vr0[0], vr1[0], vr2[0]], axis=0)
    nt = (((1,), (1,)), ((), ()))
    tn = (((0,), (0,)), ((), ()))
    s = lax.dot_general(q, k, nt, preferred_element_type=pf) * scale
    s = jnp.where(mask_ref[0] > 0, s, NEG)
    top = jnp.max(s, axis=1, keepdims=True)
    e = jnp.exp(s - top)
    p = e / jnp.sum(e, axis=1, keepdims=True)
    pb = p.astype(jnp.bfloat16)
    ob = jnp.dot(pb, v, preferred_element_type=pf).astype(jnp.bfloat16)
    out_ref[...] = ob
    delta = jnp.sum(do.astype(pf) * ob.astype(pf), axis=1, keepdims=True)
    dp = lax.dot_general(do, v, nt, preferred_element_type=pf)
    ds = p * (dp - delta)
    dsb = ds.astype(jnp.bfloat16)
    dq_ref[...] = (jnp.dot(dsb, k, preferred_element_type=pf) * scale).astype(jnp.bfloat16)
    g = 5 * BS
    rk_ref[0] = (lax.dot_general(dsb[:, g:], q, tn, preferred_element_type=pf) * scale).astype(jnp.bfloat16)
    rv_ref[0] = lax.dot_general(pb[:, g:], do, tn, preferred_element_type=pf).astype(jnp.bfloat16)
    pb_ref[0, 0] = pb[:, :g]
    dsb_ref[0, 0] = dsb[:, :g]


def terms_kernel(q_ref, do_ref, pb_ref, dsb_ref, wk_ref, wv_ref, gk_ref, gv_ref):
    pf = jnp.float32
    scale = 1.0 / math.sqrt(HD)
    tn = (((0,), (0,)), ((), ()))
    kt = lax.dot_general(dsb_ref[0, 0], q_ref[...], tn, preferred_element_type=pf) * scale
    vt = lax.dot_general(pb_ref[0, 0], do_ref[...], tn, preferred_element_type=pf)
    w = 3 * BS
    wk_ref[0] = kt[:w]
    wv_ref[0] = vt[:w]
    gk_ref[0] = kt[w:]
    gv_ref[0] = vt[w:]


def attention(query, dout, mask, padded, glob, fetched, slots):
    rows, width = query.shape
    heads = width // HD
    nbd = rows // BS
    span = (5 + R) * BS
    g = 5 * BS

    def tile(j, col):
        return pl.BlockSpec((BS, HD), lambda n, h, s: (n + j, h + col))

    def rand_tile(j, col):
        return pl.BlockSpec((1, BS, HD), lambda n, h, s: (s[n * R + j], 0, h + col))

    row_spec = pl.BlockSpec((BS, HD), lambda n, h, s: (n, h))
    in_specs = (
        [row_spec, row_spec, pl.BlockSpec((1, 1, span), lambda n, h, s: (n, 0, 0))]
        + [tile(j, 0) for j in range(3)]
        + [tile(j, heads) for j in range(3)]
        + [
            pl.BlockSpec((2 * BS, HD), lambda n, h, s: (0, h)),
            pl.BlockSpec((2 * BS, HD), lambda n, h, s: (0, h + heads)),
        ]
        + [rand_tile(j, 0) for j in range(R)]
        + [rand_tile(j, heads) for j in range(R)]
    )
    rand_spec = pl.BlockSpec((1, R * BS, HD), lambda n, h, s: (n, 0, h))
    prob_spec = pl.BlockSpec((1, 1, BS, g), lambda n, h, s: (n, h, 0, 0))
    out_specs = [row_spec, row_spec, rand_spec, rand_spec, prob_spec, prob_spec]
    out_shape = [
        jax.ShapeDtypeStruct((rows, width), jnp.bfloat16),
        jax.ShapeDtypeStruct((rows, width), jnp.bfloat16),
        jax.ShapeDtypeStruct((nbd, R * BS, width), jnp.bfloat16),
        jax.ShapeDtypeStruct((nbd, R * BS, width), jnp.bfloat16),
        jax.ShapeDtypeStruct((nbd, heads, BS, g), jnp.bfloat16),
        jax.ShapeDtypeStruct((nbd, heads, BS, g), jnp.bfloat16),
    ]
    grid_spec = pltpu.PrefetchScalarGridSpec(
        num_scalar_prefetch=1,
        grid=(nbd, heads),
        in_specs=in_specs,
        out_specs=out_specs,
    )
    args = [query, dout, mask] + [padded] * 6 + [glob] * 2 + [fetched] * (2 * R)
    out, dq, rk, rv, pb, dsb = pl.pallas_call(
        scores_kernel,
        grid_spec=grid_spec,
        out_shape=out_shape,
        interpret=INTERPRET,
    )(slots, *args)

    row2 = pl.BlockSpec((BS, HD), lambda n, h: (n, h))
    prob2 = pl.BlockSpec((1, 1, BS, g), lambda n, h: (n, h, 0, 0))

    def term_spec(size):
        return pl.BlockSpec((1, size, HD), lambda n, h: (n, 0, h))

    wk, wv, gk, gv = pl.pallas_call(
        terms_kernel,
        grid=(nbd, heads),
        in_specs=[row2, row2, prob2, prob2],
        out_specs=[term_spec(3 * BS), term_spec(3 * BS), term_spec(2 * BS), term_spec(2 * BS)],
        out_shape=[
            jax.ShapeDtypeStruct((nbd, 3 * BS, width), jnp.float32),
            jax.ShapeDtypeStruct((nbd, 3 * BS, width), jnp.float32),
            jax.ShapeDtypeStruct((nbd, 2 * BS, width), jnp.float32),
            jax.ShapeDtypeStruct((nbd, 2 * BS, width), jnp.float32),
        ],
        interpret=INTERPRET,
    )(query, dout, pb, dsb)
    return out, dq, wk, wv, gk, gv, rk, rv


def overlap(terms, nbd):
    width = terms.shape[-1]
    w4 = terms.reshape(nbd, 3, BS, width)
    return (
        jnp.pad(w4[:, 0], ((0, 2), (0, 0), (0, 0)))
        + jnp.pad(w4[:, 1], ((1, 1), (0, 0), (0, 0)))
        + jnp.pad(w4[:, 2], ((2, 0), (0, 0), (0, 0)))
    )


def body(query, key, value, dout, rand):
    rows, width = query.shape
    ndev = lax.axis_size(("head", "blk"))
    me = lax.axis_index(("head", "blk"))
    nbd = rows // BS
    total = nbd * ndev
    cap = (R * nbd + ndev - 1) // ndev
    pf = jnp.float32
    span = (5 + R) * BS
    pair = jnp.concatenate([key, value], axis=1)
    padded = extended(pair, ((("head", "blk"), 0),), BS)
    glob = from_root(pair[: 2 * BS], ("head", "blk"), 0)
    flat = rand.reshape(ndev, nbd * R)
    owner = flat // nbd
    local = flat - owner * nbd
    hit = owner == me
    order = jnp.cumsum(hit.astype(jnp.int32), axis=1) - 1
    slot_ids = jnp.arange(cap, dtype=jnp.int32)
    chosen = hit[:, None, :] & (order[:, None, :] == slot_ids[None, :, None])
    block_id = jnp.sum(jnp.where(chosen, local[:, None, :], 0), axis=2).reshape(-1)
    filled = jnp.any(chosen, axis=2).reshape(-1)
    tiles = pair.reshape(nbd, BS, 2 * width)
    outgoing = jnp.where(
        filled[:, None, None], jnp.take(tiles, block_id, axis=0), jnp.zeros((), pair.dtype)
    )
    fetched = lax.all_to_all(outgoing, ("head", "blk"), split_axis=0, concat_axis=0, tiled=True)
    mine = lax.dynamic_slice_in_dim(rand, me * nbd, nbd, 0).reshape(-1)
    mine_owner = mine // nbd
    count = mine.shape[0]
    earlier = jnp.arange(count)[:, None] > jnp.arange(count)[None, :]
    same = mine_owner[:, None] == mine_owner[None, :]
    mine_rank = jnp.sum(earlier & same, axis=1)
    mine_slot = (mine_owner * cap + mine_rank).astype(jnp.int32)
    first = me * nbd + jnp.arange(nbd, dtype=jnp.int32)
    always = first >= 0
    valid = jnp.concatenate(
        [
            jnp.stack([first > 0, always, first < total - 1, always, always], axis=1),
            jnp.ones((nbd, R), bool),
        ],
        axis=1,
    )
    mask = jnp.repeat(valid, BS, axis=1).astype(pf).reshape(nbd, 1, span)
    out, dq, wk, wv, gk, gv, rk, rv = attention(query, dout, mask, padded, glob, fetched, mine_slot)
    sk = overlap(wk, nbd)
    sv = overlap(wv, nbd)
    rims = jnp.concatenate(
        [
            jnp.concatenate([sk[0], sv[0]], axis=-1),
            jnp.concatenate([sk[nbd + 1], sv[nbd + 1]], axis=-1),
        ],
        axis=0,
    )
    arrived = extended(rims.astype(jnp.bfloat16), ((("head", "blk"), 0),), BS).astype(pf)
    own = jnp.concatenate([sk[1 : nbd + 1], sv[1 : nbd + 1]], axis=-1)
    own = own.at[0].add(arrived[:BS]).at[nbd - 1].add(arrived[3 * BS :])
    glob_grad = jnp.concatenate([jnp.sum(gk, axis=0), jnp.sum(gv, axis=0)], axis=-1).reshape(
        2, BS, 2 * width
    )
    glob_total = lax.psum(glob_grad.astype(jnp.bfloat16), ("head", "blk")).astype(pf)
    own = own.at[:2].add(jnp.where(me == 0, glob_total, 0.0))
    rand_grad = jnp.concatenate([rk, rv], axis=-1).reshape(nbd * R, BS, 2 * width)
    match = mine_slot[None, :] == jnp.arange(ndev * cap, dtype=jnp.int32)[:, None]
    source = jnp.argmax(match, axis=1)
    returning = jnp.where(
        jnp.any(match, axis=1)[:, None, None],
        jnp.take(rand_grad, source, axis=0),
        jnp.zeros((), jnp.bfloat16),
    )
    back = lax.all_to_all(returning, ("head", "blk"), split_axis=0, concat_axis=0, tiled=True)
    onehot = (
        (block_id[None, :] == jnp.arange(nbd, dtype=jnp.int32)[:, None]) & filled[None, :]
    ).astype(jnp.bfloat16)
    own = own + jnp.dot(
        onehot, back.reshape(ndev * cap, BS * 2 * width), preferred_element_type=pf
    ).reshape(nbd, BS, 2 * width)
    dk = own[..., :width].astype(jnp.bfloat16).reshape(rows, width)
    dv = own[..., width:].astype(jnp.bfloat16).reshape(rows, width)
    return (out, dq, dk, dv)


def solution(mesh):
    placed = (
        P(("dp", "head", "blk"), None),
        P(("dp", "head", "blk"), None),
        P(("dp", "head", "blk"), None),
        P(("dp", "head", "blk"), None),
        P("dp", None),
    )
    return jax.shard_map(
        body,
        mesh=mesh,
        in_specs=placed,
        out_specs=(
            P(("dp", "head", "blk"), None),
            P(("dp", "head", "blk"), None),
            P(("dp", "head", "blk"), None),
            P(("dp", "head", "blk"), None),
        ),
        check_vma=False,
    )
```

```python
import math

import jax
import jax.numpy as jnp
from jax import lax
from jax.experimental import pallas as pl
from jax.experimental.pallas import tpu as pltpu
from jax.sharding import PartitionSpec as P

HD = 128
BS = 64
R = 3


NEG = -1e30
INTERPRET = False
HG = 4


def extended(block, sides, width):
    for axis, dim in sides:
        count = lax.axis_size(axis)
        forward = [(i, i + 1) for i in range(count - 1)]
        backward = [(target, source) for source, target in forward]
        low = lax.ppermute(
            lax.slice_in_dim(block, block.shape[dim] - width, None, axis=dim), axis, forward
        )
        high = lax.ppermute(lax.slice_in_dim(block, 0, width, axis=dim), axis, backward)
        block = jnp.concatenate([low, block, high], axis=dim)
    return block


def from_root(value, axis, source):
    kept = jnp.where(lax.axis_index(axis) == source, value, 0).astype(value.dtype)
    return lax.psum(kept, axis)


def scores_kernel(
    slots_ref, q_ref, do_ref, mask_ref,
    kw0, kw1, kw2, vw0, vw1, vw2, kg, vg, kr0, kr1, kr2, vr0, vr1, vr2,
    out_ref, dq_ref, rk_ref, rv_ref, pb_ref, dsb_ref,
):
    pf = jnp.float32
    scale = 1.0 / math.sqrt(HD)
    nt = (((1,), (1,)), ((), ()))
    tn = (((0,), (0,)), ((), ()))
    g = 5 * BS
    valid = mask_ref[0] > 0
    for t in range(HG):
        c = slice(t * HD, (t + 1) * HD)
        q = q_ref[:, c]
        do = do_ref[:, c]
        k = jnp.concatenate(
            [kw0[:, c], kw1[:, c], kw2[:, c], kg[:, c], kr0[0, :, c], kr1[0, :, c], kr2[0, :, c]], axis=0
        )
        v = jnp.concatenate(
            [vw0[:, c], vw1[:, c], vw2[:, c], vg[:, c], vr0[0, :, c], vr1[0, :, c], vr2[0, :, c]], axis=0
        )
        s = lax.dot_general(q, k, nt, preferred_element_type=pf) * scale
        s = jnp.where(valid, s, NEG)
        top = jnp.max(s, axis=1, keepdims=True)
        e = jnp.exp(s - top)
        p = e / jnp.sum(e, axis=1, keepdims=True)
        pb = p.astype(jnp.bfloat16)
        ob = jnp.dot(pb, v, preferred_element_type=pf).astype(jnp.bfloat16)
        out_ref[:, c] = ob
        delta = jnp.sum(do.astype(pf) * ob.astype(pf), axis=1, keepdims=True)
        dp = lax.dot_general(do, v, nt, preferred_element_type=pf)
        ds = p * (dp - delta)
        dsb = ds.astype(jnp.bfloat16)
        dq_ref[:, c] = (jnp.dot(dsb, k, preferred_element_type=pf) * scale).astype(jnp.bfloat16)
        rk_ref[0, :, c] = (
            lax.dot_general(dsb[:, g:], q, tn, preferred_element_type=pf) * scale
        ).astype(jnp.bfloat16)
        rv_ref[0, :, c] = lax.dot_general(pb[:, g:], do, tn, preferred_element_type=pf).astype(jnp.bfloat16)
        pb_ref[0, t] = pb[:, :g]
        dsb_ref[0, t] = dsb[:, :g]


def terms_kernel(q_ref, do_ref, pb_ref, dsb_ref, wk_ref, wv_ref, gk_ref, gv_ref):
    pf = jnp.float32
    scale = 1.0 / math.sqrt(HD)
    tn = (((0,), (0,)), ((), ()))
    w = 3 * BS
    for t in range(HG):
        c = slice(t * HD, (t + 1) * HD)
        kt = lax.dot_general(dsb_ref[0, t], q_ref[:, c], tn, preferred_element_type=pf) * scale
        vt = lax.dot_general(pb_ref[0, t], do_ref[:, c], tn, preferred_element_type=pf)
        wk_ref[0, :, c] = kt[:w]
        wv_ref[0, :, c] = vt[:w]
        gk_ref[0, :, c] = kt[w:]
        gv_ref[0, :, c] = vt[w:]


def attention(query, dout, mask, padded, glob, fetched, slots):
    rows, width = query.shape
    heads = width // HD
    groups = heads // HG
    cw = HG * HD
    nbd = rows // BS
    span = (5 + R) * BS
    g = 5 * BS

    def tile(j, col):
        return pl.BlockSpec((BS, cw), lambda n, h, s: (n + j, h + col))

    def rand_tile(j, col):
        return pl.BlockSpec((1, BS, cw), lambda n, h, s: (s[n * R + j], 0, h + col))

    row_spec = pl.BlockSpec((BS, cw), lambda n, h, s: (n, h))
    in_specs = (
        [row_spec, row_spec, pl.BlockSpec((1, 1, span), lambda n, h, s: (n, 0, 0))]
        + [tile(j, 0) for j in range(3)]
        + [tile(j, groups) for j in range(3)]
        + [
            pl.BlockSpec((2 * BS, cw), lambda n, h, s: (0, h)),
            pl.BlockSpec((2 * BS, cw), lambda n, h, s: (0, h + groups)),
        ]
        + [rand_tile(j, 0) for j in range(R)]
        + [rand_tile(j, groups) for j in range(R)]
    )
    rand_spec = pl.BlockSpec((1, R * BS, cw), lambda n, h, s: (n, 0, h))
    prob_spec = pl.BlockSpec((1, HG, BS, g), lambda n, h, s: (n, h, 0, 0))
    out_specs = [row_spec, row_spec, rand_spec, rand_spec, prob_spec, prob_spec]
    out_shape = [
        jax.ShapeDtypeStruct((rows, width), jnp.bfloat16),
        jax.ShapeDtypeStruct((rows, width), jnp.bfloat16),
        jax.ShapeDtypeStruct((nbd, R * BS, width), jnp.bfloat16),
        jax.ShapeDtypeStruct((nbd, R * BS, width), jnp.bfloat16),
        jax.ShapeDtypeStruct((nbd, heads, BS, g), jnp.bfloat16),
        jax.ShapeDtypeStruct((nbd, heads, BS, g), jnp.bfloat16),
    ]
    grid_spec = pltpu.PrefetchScalarGridSpec(
        num_scalar_prefetch=1,
        grid=(nbd, groups),
        in_specs=in_specs,
        out_specs=out_specs,
    )
    args = [query, dout, mask] + [padded] * 6 + [glob] * 2 + [fetched] * (2 * R)
    out, dq, rk, rv, pb, dsb = pl.pallas_call(
        scores_kernel,
        grid_spec=grid_spec,
        out_shape=out_shape,
        interpret=INTERPRET,
    )(slots, *args)

    row2 = pl.BlockSpec((BS, cw), lambda n, h: (n, h))
    prob2 = pl.BlockSpec((1, HG, BS, g), lambda n, h: (n, h, 0, 0))

    def term_spec(size):
        return pl.BlockSpec((1, size, cw), lambda n, h: (n, 0, h))

    wk, wv, gk, gv = pl.pallas_call(
        terms_kernel,
        grid=(nbd, groups),
        in_specs=[row2, row2, prob2, prob2],
        out_specs=[term_spec(3 * BS), term_spec(3 * BS), term_spec(2 * BS), term_spec(2 * BS)],
        out_shape=[
            jax.ShapeDtypeStruct((nbd, 3 * BS, width), jnp.float32),
            jax.ShapeDtypeStruct((nbd, 3 * BS, width), jnp.float32),
            jax.ShapeDtypeStruct((nbd, 2 * BS, width), jnp.float32),
            jax.ShapeDtypeStruct((nbd, 2 * BS, width), jnp.float32),
        ],
        interpret=INTERPRET,
    )(query, dout, pb, dsb)
    return out, dq, wk, wv, gk, gv, rk, rv


def overlap(terms, nbd):
    width = terms.shape[-1]
    w4 = terms.reshape(nbd, 3, BS, width)
    return (
        jnp.pad(w4[:, 0], ((0, 2), (0, 0), (0, 0)))
        + jnp.pad(w4[:, 1], ((1, 1), (0, 0), (0, 0)))
        + jnp.pad(w4[:, 2], ((2, 0), (0, 0), (0, 0)))
    )


def body(query, key, value, dout, rand):
    rows, width = query.shape
    ndev = lax.axis_size(("head", "blk"))
    me = lax.axis_index(("head", "blk"))
    nbd = rows // BS
    total = nbd * ndev
    cap = (R * nbd + ndev - 1) // ndev
    pf = jnp.float32
    span = (5 + R) * BS
    pair = jnp.concatenate([key, value], axis=1)
    padded = extended(pair, ((("head", "blk"), 0),), BS)
    glob = from_root(pair[: 2 * BS], ("head", "blk"), 0)
    flat = rand.reshape(ndev, nbd * R)
    owner = flat // nbd
    local = flat - owner * nbd
    hit = owner == me
    order = jnp.cumsum(hit.astype(jnp.int32), axis=1) - 1
    slot_ids = jnp.arange(cap, dtype=jnp.int32)
    chosen = hit[:, None, :] & (order[:, None, :] == slot_ids[None, :, None])
    block_id = jnp.sum(jnp.where(chosen, local[:, None, :], 0), axis=2).reshape(-1)
    filled = jnp.any(chosen, axis=2).reshape(-1)
    tiles = pair.reshape(nbd, BS, 2 * width)
    outgoing = jnp.where(
        filled[:, None, None], jnp.take(tiles, block_id, axis=0), jnp.zeros((), pair.dtype)
    )
    fetched = lax.all_to_all(outgoing, ("head", "blk"), split_axis=0, concat_axis=0, tiled=True)
    mine = lax.dynamic_slice_in_dim(rand, me * nbd, nbd, 0).reshape(-1)
    mine_owner = mine // nbd
    count = mine.shape[0]
    earlier = jnp.arange(count)[:, None] > jnp.arange(count)[None, :]
    same = mine_owner[:, None] == mine_owner[None, :]
    mine_rank = jnp.sum(earlier & same, axis=1)
    mine_slot = (mine_owner * cap + mine_rank).astype(jnp.int32)
    first = me * nbd + jnp.arange(nbd, dtype=jnp.int32)
    always = first >= 0
    valid = jnp.concatenate(
        [
            jnp.stack([first > 0, always, first < total - 1, always, always], axis=1),
            jnp.ones((nbd, R), bool),
        ],
        axis=1,
    )
    mask = jnp.repeat(valid, BS, axis=1).astype(pf).reshape(nbd, 1, span)
    out, dq, wk, wv, gk, gv, rk, rv = attention(query, dout, mask, padded, glob, fetched, mine_slot)
    sk = overlap(wk, nbd)
    sv = overlap(wv, nbd)
    rims = jnp.concatenate(
        [
            jnp.concatenate([sk[0], sv[0]], axis=-1),
            jnp.concatenate([sk[nbd + 1], sv[nbd + 1]], axis=-1),
        ],
        axis=0,
    )
    arrived = extended(rims.astype(jnp.bfloat16), ((("head", "blk"), 0),), BS).astype(pf)
    own = jnp.concatenate([sk[1 : nbd + 1], sv[1 : nbd + 1]], axis=-1)
    glob_grad = jnp.concatenate([jnp.sum(gk, axis=0), jnp.sum(gv, axis=0)], axis=-1).reshape(
        2, BS, 2 * width
    )
    glob_total = lax.psum(glob_grad.astype(jnp.bfloat16), ("head", "blk")).astype(pf)
    edge = jnp.concatenate(
        [arrived[None, :BS], jnp.zeros((nbd - 2, BS, 2 * width), pf), arrived[None, 3 * BS :]], axis=0
    )
    lead = jnp.pad(jnp.where(me == 0, glob_total, 0.0), ((0, nbd - 2), (0, 0), (0, 0)))
    own = own + edge + lead
    rand_grad = jnp.concatenate([rk, rv], axis=-1).reshape(nbd * R, BS, 2 * width)
    match = mine_slot[None, :] == jnp.arange(ndev * cap, dtype=jnp.int32)[:, None]
    source = jnp.argmax(match, axis=1)
    returning = jnp.where(
        jnp.any(match, axis=1)[:, None, None],
        jnp.take(rand_grad, source, axis=0),
        jnp.zeros((), jnp.bfloat16),
    )
    back = lax.all_to_all(returning, ("head", "blk"), split_axis=0, concat_axis=0, tiled=True)
    onehot = (
        (block_id[None, :] == jnp.arange(nbd, dtype=jnp.int32)[:, None]) & filled[None, :]
    ).astype(jnp.bfloat16)
    own = own + jnp.dot(
        onehot, back.reshape(ndev * cap, BS * 2 * width), preferred_element_type=pf
    ).reshape(nbd, BS, 2 * width)
    dk = own[..., :width].astype(jnp.bfloat16).reshape(rows, width)
    dv = own[..., width:].astype(jnp.bfloat16).reshape(rows, width)
    return (out, dq, dk, dv)


def solution(mesh):
    placed = (
        P(("dp", "head", "blk"), None),
        P(("dp", "head", "blk"), None),
        P(("dp", "head", "blk"), None),
        P(("dp", "head", "blk"), None),
        P("dp", None),
    )
    return jax.shard_map(
        body,
        mesh=mesh,
        in_specs=placed,
        out_specs=(
            P(("dp", "head", "blk"), None),
            P(("dp", "head", "blk"), None),
            P(("dp", "head", "blk"), None),
            P(("dp", "head", "blk"), None),
        ),
        check_vma=False,
    )
```

```python
import math

import jax
import jax.numpy as jnp
from jax import lax
from jax.experimental import pallas as pl
from jax.experimental.pallas import tpu as pltpu
from jax.sharding import PartitionSpec as P

HD = 128
BS = 64
R = 3


NEG = -1e30
INTERPRET = False
HG = 4
CHUNKS = 2


def extended(block, sides, width):
    for axis, dim in sides:
        count = lax.axis_size(axis)
        forward = [(i, i + 1) for i in range(count - 1)]
        backward = [(target, source) for source, target in forward]
        low = lax.ppermute(
            lax.slice_in_dim(block, block.shape[dim] - width, None, axis=dim), axis, forward
        )
        high = lax.ppermute(lax.slice_in_dim(block, 0, width, axis=dim), axis, backward)
        block = jnp.concatenate([low, block, high], axis=dim)
    return block


def from_root(value, axis, source):
    kept = jnp.where(lax.axis_index(axis) == source, value, 0).astype(value.dtype)
    return lax.psum(kept, axis)


def scores_kernel(
    slots_ref, q_ref, do_ref, mask_ref,
    kw0, kw1, kw2, vw0, vw1, vw2, kg, vg, kr0, kr1, kr2, vr0, vr1, vr2,
    out_ref, dq_ref, rk_ref, rv_ref, pb_ref, dsb_ref,
):
    pf = jnp.float32
    scale = 1.0 / math.sqrt(HD)
    nt = (((1,), (1,)), ((), ()))
    tn = (((0,), (0,)), ((), ()))
    g = 5 * BS
    valid = mask_ref[0] > 0
    for t in range(HG):
        c = slice(t * HD, (t + 1) * HD)
        q = q_ref[:, c]
        do = do_ref[:, c]
        k = jnp.concatenate(
            [kw0[:, c], kw1[:, c], kw2[:, c], kg[:, c], kr0[0, :, c], kr1[0, :, c], kr2[0, :, c]], axis=0
        )
        v = jnp.concatenate(
            [vw0[:, c], vw1[:, c], vw2[:, c], vg[:, c], vr0[0, :, c], vr1[0, :, c], vr2[0, :, c]], axis=0
        )
        s = lax.dot_general(q, k, nt, preferred_element_type=pf) * scale
        s = jnp.where(valid, s, NEG)
        top = jnp.max(s, axis=1, keepdims=True)
        e = jnp.exp(s - top)
        p = e / jnp.sum(e, axis=1, keepdims=True)
        pb = p.astype(jnp.bfloat16)
        ob = jnp.dot(pb, v, preferred_element_type=pf).astype(jnp.bfloat16)
        out_ref[:, c] = ob
        delta = jnp.sum(do.astype(pf) * ob.astype(pf), axis=1, keepdims=True)
        dp = lax.dot_general(do, v, nt, preferred_element_type=pf)
        ds = p * (dp - delta)
        dsb = ds.astype(jnp.bfloat16)
        dq_ref[:, c] = (jnp.dot(dsb, k, preferred_element_type=pf) * scale).astype(jnp.bfloat16)
        rk_ref[0, :, c] = (
            lax.dot_general(dsb[:, g:], q, tn, preferred_element_type=pf) * scale
        ).astype(jnp.bfloat16)
        rv_ref[0, :, c] = lax.dot_general(pb[:, g:], do, tn, preferred_element_type=pf).astype(jnp.bfloat16)
        pb_ref[0, t] = pb[:, :g]
        dsb_ref[0, t] = dsb[:, :g]


def terms_kernel(q_ref, do_ref, pb_ref, dsb_ref, wk_ref, wv_ref, gk_ref, gv_ref):
    pf = jnp.float32
    scale = 1.0 / math.sqrt(HD)
    tn = (((0,), (0,)), ((), ()))
    w = 3 * BS
    for t in range(HG):
        c = slice(t * HD, (t + 1) * HD)
        kt = lax.dot_general(dsb_ref[0, t], q_ref[:, c], tn, preferred_element_type=pf) * scale
        vt = lax.dot_general(pb_ref[0, t], do_ref[:, c], tn, preferred_element_type=pf)
        wk_ref[0, :, c] = kt[:w]
        wv_ref[0, :, c] = vt[:w]
        gk_ref[0, :, c] = kt[w:]
        gv_ref[0, :, c] = vt[w:]


def attention(query, dout, mask, padded, glob, fetched, slots, chunk, chunks):
    rows, width = query.shape
    heads = width // HD
    groups = heads // HG
    per = groups // chunks
    base = chunk * per
    cw = HG * HD
    part = per * cw
    nbd = rows // BS
    span = (5 + R) * BS
    g = 5 * BS
    hc = per * HG

    def tile(j, col):
        return pl.BlockSpec((BS, cw), lambda n, h, s: (n + j, h + col))

    def rand_tile(j, col):
        return pl.BlockSpec((1, BS, cw), lambda n, h, s: (s[n * R + j], 0, h + col))

    row_spec = pl.BlockSpec((BS, cw), lambda n, h, s: (n, h + base))
    in_specs = (
        [row_spec, row_spec, pl.BlockSpec((1, 1, span), lambda n, h, s: (n, 0, 0))]
        + [tile(j, base) for j in range(3)]
        + [tile(j, groups + base) for j in range(3)]
        + [
            pl.BlockSpec((2 * BS, cw), lambda n, h, s: (0, h + base)),
            pl.BlockSpec((2 * BS, cw), lambda n, h, s: (0, h + groups + base)),
        ]
        + [rand_tile(j, 0) for j in range(R)]
        + [rand_tile(j, per) for j in range(R)]
    )
    own_row = pl.BlockSpec((BS, cw), lambda n, h, s: (n, h))
    rand_spec = pl.BlockSpec((1, R * BS, cw), lambda n, h, s: (n, 0, h))
    prob_spec = pl.BlockSpec((1, HG, BS, g), lambda n, h, s: (n, h, 0, 0))
    out_specs = [own_row, own_row, rand_spec, rand_spec, prob_spec, prob_spec]
    out_shape = [
        jax.ShapeDtypeStruct((rows, part), jnp.bfloat16),
        jax.ShapeDtypeStruct((rows, part), jnp.bfloat16),
        jax.ShapeDtypeStruct((nbd, R * BS, part), jnp.bfloat16),
        jax.ShapeDtypeStruct((nbd, R * BS, part), jnp.bfloat16),
        jax.ShapeDtypeStruct((nbd, hc, BS, g), jnp.bfloat16),
        jax.ShapeDtypeStruct((nbd, hc, BS, g), jnp.bfloat16),
    ]
    grid_spec = pltpu.PrefetchScalarGridSpec(
        num_scalar_prefetch=1,
        grid=(nbd, per),
        in_specs=in_specs,
        out_specs=out_specs,
    )
    args = [query, dout, mask] + [padded] * 6 + [glob] * 2 + [fetched] * (2 * R)
    out, dq, rk, rv, pb, dsb = pl.pallas_call(
        scores_kernel,
        grid_spec=grid_spec,
        out_shape=out_shape,
        interpret=INTERPRET,
    )(slots, *args)

    row2 = pl.BlockSpec((BS, cw), lambda n, h: (n, h + base))
    prob2 = pl.BlockSpec((1, HG, BS, g), lambda n, h: (n, h, 0, 0))

    def term_spec(size):
        return pl.BlockSpec((1, size, cw), lambda n, h: (n, 0, h))

    wk, wv, gk, gv = pl.pallas_call(
        terms_kernel,
        grid=(nbd, per),
        in_specs=[row2, row2, prob2, prob2],
        out_specs=[term_spec(3 * BS), term_spec(3 * BS), term_spec(2 * BS), term_spec(2 * BS)],
        out_shape=[
            jax.ShapeDtypeStruct((nbd, 3 * BS, part), jnp.float32),
            jax.ShapeDtypeStruct((nbd, 3 * BS, part), jnp.float32),
            jax.ShapeDtypeStruct((nbd, 2 * BS, part), jnp.float32),
            jax.ShapeDtypeStruct((nbd, 2 * BS, part), jnp.float32),
        ],
        interpret=INTERPRET,
    )(query, dout, pb, dsb)
    return out, dq, wk, wv, gk, gv, rk, rv


def overlap(terms, nbd):
    width = terms.shape[-1]
    w4 = terms.reshape(nbd, 3, BS, width)
    return (
        jnp.pad(w4[:, 0], ((0, 2), (0, 0), (0, 0)))
        + jnp.pad(w4[:, 1], ((1, 1), (0, 0), (0, 0)))
        + jnp.pad(w4[:, 2], ((2, 0), (0, 0), (0, 0)))
    )


def body(query, key, value, dout, rand):
    rows, width = query.shape
    ndev = lax.axis_size(("head", "blk"))
    me = lax.axis_index(("head", "blk"))
    nbd = rows // BS
    total = nbd * ndev
    cap = (R * nbd + ndev - 1) // ndev
    pf = jnp.float32
    span = (5 + R) * BS
    pair = jnp.concatenate([key, value], axis=1)
    padded = extended(pair, ((("head", "blk"), 0),), BS)
    glob = from_root(pair[: 2 * BS], ("head", "blk"), 0)
    flat = rand.reshape(ndev, nbd * R)
    owner = flat // nbd
    local = flat - owner * nbd
    hit = owner == me
    order = jnp.cumsum(hit.astype(jnp.int32), axis=1) - 1
    slot_ids = jnp.arange(cap, dtype=jnp.int32)
    chosen = hit[:, None, :] & (order[:, None, :] == slot_ids[None, :, None])
    block_id = jnp.sum(jnp.where(chosen, local[:, None, :], 0), axis=2).reshape(-1)
    filled = jnp.any(chosen, axis=2).reshape(-1)
    tiles = pair.reshape(nbd, BS, 2 * width)
    outgoing = jnp.where(
        filled[:, None, None], jnp.take(tiles, block_id, axis=0), jnp.zeros((), pair.dtype)
    )
    mine = lax.dynamic_slice_in_dim(rand, me * nbd, nbd, 0).reshape(-1)
    mine_owner = mine // nbd
    count = mine.shape[0]
    earlier = jnp.arange(count)[:, None] > jnp.arange(count)[None, :]
    same = mine_owner[:, None] == mine_owner[None, :]
    mine_rank = jnp.sum(earlier & same, axis=1)
    mine_slot = (mine_owner * cap + mine_rank).astype(jnp.int32)
    first = me * nbd + jnp.arange(nbd, dtype=jnp.int32)
    always = first >= 0
    valid = jnp.concatenate(
        [
            jnp.stack([first > 0, always, first < total - 1, always, always], axis=1),
            jnp.ones((nbd, R), bool),
        ],
        axis=1,
    )
    mask = jnp.repeat(valid, BS, axis=1).astype(pf).reshape(nbd, 1, span)
    match = mine_slot[None, :] == jnp.arange(ndev * cap, dtype=jnp.int32)[:, None]
    source = jnp.argmax(match, axis=1)
    present = jnp.any(match, axis=1)[:, None, None]
    onehot = (
        (block_id[None, :] == jnp.arange(nbd, dtype=jnp.int32)[:, None]) & filled[None, :]
    ).astype(jnp.bfloat16)
    chunks = CHUNKS
    part = width // chunks
    results = []
    previous = None
    for c in range(chunks):
        cols = jnp.concatenate(
            [outgoing[..., c * part : (c + 1) * part], outgoing[..., width + c * part : width + (c + 1) * part]],
            axis=-1,
        )
        if previous is not None:
            cols, _ = lax.optimization_barrier((cols, previous))
        fetched = lax.all_to_all(cols, ("head", "blk"), split_axis=0, concat_axis=0, tiled=True)
        previous = fetched
        out, dq, wk, wv, gk, gv, rk, rv = attention(
            query, dout, mask, padded, glob, fetched, mine_slot, c, chunks
        )
        sk = overlap(wk, nbd)
        sv = overlap(wv, nbd)
        rims = jnp.concatenate(
            [
                jnp.concatenate([sk[0], sv[0]], axis=-1),
                jnp.concatenate([sk[nbd + 1], sv[nbd + 1]], axis=-1),
            ],
            axis=0,
        )
        arrived = extended(rims.astype(jnp.bfloat16), ((("head", "blk"), 0),), BS).astype(pf)
        own = jnp.concatenate([sk[1 : nbd + 1], sv[1 : nbd + 1]], axis=-1)
        glob_grad = jnp.concatenate([jnp.sum(gk, axis=0), jnp.sum(gv, axis=0)], axis=-1).reshape(
            2, BS, 2 * part
        )
        glob_total = lax.psum(glob_grad.astype(jnp.bfloat16), ("head", "blk")).astype(pf)
        edge = jnp.concatenate(
            [arrived[None, :BS], jnp.zeros((nbd - 2, BS, 2 * part), pf), arrived[None, 3 * BS :]], axis=0
        )
        lead = jnp.pad(jnp.where(me == 0, glob_total, 0.0), ((0, nbd - 2), (0, 0), (0, 0)))
        own = own + edge + lead
        rand_grad = jnp.concatenate([rk, rv], axis=-1).reshape(nbd * R, BS, 2 * part)
        returning = jnp.where(present, jnp.take(rand_grad, source, axis=0), jnp.zeros((), jnp.bfloat16))
        back = lax.all_to_all(returning, ("head", "blk"), split_axis=0, concat_axis=0, tiled=True)
        own = own + jnp.dot(
            onehot, back.reshape(ndev * cap, BS * 2 * part), preferred_element_type=pf
        ).reshape(nbd, BS, 2 * part)
        dk = own[..., :part].astype(jnp.bfloat16).reshape(rows, part)
        dv = own[..., part:].astype(jnp.bfloat16).reshape(rows, part)
        results.append((out, dq, dk, dv))
    return tuple(jnp.concatenate([r[i] for r in results], axis=1) for i in range(4))


def solution(mesh):
    placed = (
        P(("dp", "head", "blk"), None),
        P(("dp", "head", "blk"), None),
        P(("dp", "head", "blk"), None),
        P(("dp", "head", "blk"), None),
        P("dp", None),
    )
    return jax.shard_map(
        body,
        mesh=mesh,
        in_specs=placed,
        out_specs=(
            P(("dp", "head", "blk"), None),
            P(("dp", "head", "blk"), None),
            P(("dp", "head", "blk"), None),
            P(("dp", "head", "blk"), None),
        ),
        check_vma=False,
    )
```

```python
import math

import jax
import jax.numpy as jnp
from jax import lax
from jax.experimental import pallas as pl
from jax.experimental.pallas import tpu as pltpu
from jax.sharding import PartitionSpec as P

HD = 128
BS = 64
R = 3


NEG = -1e30
INTERPRET = False
HG = 4
CHUNKS = 2


def extended(block, sides, width):
    for axis, dim in sides:
        count = lax.axis_size(axis)
        forward = [(i, i + 1) for i in range(count - 1)]
        backward = [(target, source) for source, target in forward]
        low = lax.ppermute(
            lax.slice_in_dim(block, block.shape[dim] - width, None, axis=dim), axis, forward
        )
        high = lax.ppermute(lax.slice_in_dim(block, 0, width, axis=dim), axis, backward)
        block = jnp.concatenate([low, block, high], axis=dim)
    return block


def from_root(value, axis, source):
    kept = jnp.where(lax.axis_index(axis) == source, value, 0).astype(value.dtype)
    return lax.psum(kept, axis)


def scores_kernel(
    slots_ref, q_ref, do_ref, mask_ref,
    kw0, kw1, kw2, vw0, vw1, vw2, kg, vg, kr0, kr1, kr2, vr0, vr1, vr2,
    out_ref, dq_ref, rk_ref, rv_ref, pb_ref, dsb_ref,
):
    pf = jnp.float32
    scale = 1.0 / math.sqrt(HD)
    nt = (((1,), (1,)), ((), ()))
    tn = (((0,), (0,)), ((), ()))
    g = 5 * BS
    valid = mask_ref[0] > 0
    for t in range(HG):
        c = slice(t * HD, (t + 1) * HD)
        q = q_ref[:, c]
        do = do_ref[:, c]
        k = jnp.concatenate(
            [kw0[:, c], kw1[:, c], kw2[:, c], kg[:, c], kr0[0, :, c], kr1[0, :, c], kr2[0, :, c]], axis=0
        )
        v = jnp.concatenate(
            [vw0[:, c], vw1[:, c], vw2[:, c], vg[:, c], vr0[0, :, c], vr1[0, :, c], vr2[0, :, c]], axis=0
        )
        s = lax.dot_general(q, k, nt, preferred_element_type=pf) * scale
        s = jnp.where(valid, s, NEG)
        top = jnp.max(s, axis=1, keepdims=True)
        e = jnp.exp(s - top)
        p = e / jnp.sum(e, axis=1, keepdims=True)
        pb = p.astype(jnp.bfloat16)
        ob = jnp.dot(pb, v, preferred_element_type=pf).astype(jnp.bfloat16)
        out_ref[:, c] = ob
        delta = jnp.sum(do.astype(pf) * ob.astype(pf), axis=1, keepdims=True)
        dp = lax.dot_general(do, v, nt, preferred_element_type=pf)
        ds = p * (dp - delta)
        dsb = ds.astype(jnp.bfloat16)
        dq_ref[:, c] = (jnp.dot(dsb, k, preferred_element_type=pf) * scale).astype(jnp.bfloat16)
        rk_ref[0, :, c] = (
            lax.dot_general(dsb[:, g:], q, tn, preferred_element_type=pf) * scale
        ).astype(jnp.bfloat16)
        rv_ref[0, :, c] = lax.dot_general(pb[:, g:], do, tn, preferred_element_type=pf).astype(jnp.bfloat16)
        pb_ref[0, t] = pb[:, :g]
        dsb_ref[0, t] = dsb[:, :g]


def terms_kernel(q_ref, do_ref, pb_ref, dsb_ref, wk_ref, wv_ref, gk_ref, gv_ref):
    pf = jnp.float32
    scale = 1.0 / math.sqrt(HD)
    tn = (((0,), (0,)), ((), ()))
    w = 3 * BS
    for t in range(HG):
        c = slice(t * HD, (t + 1) * HD)
        kt = lax.dot_general(dsb_ref[0, t], q_ref[:, c], tn, preferred_element_type=pf) * scale
        vt = lax.dot_general(pb_ref[0, t], do_ref[:, c], tn, preferred_element_type=pf)
        wk_ref[0, :, c] = kt[:w]
        wv_ref[0, :, c] = vt[:w]
        gk_ref[0, :, c] = kt[w:]
        gv_ref[0, :, c] = vt[w:]


def attention(query, dout, mask, padded, glob, fetched, slots, chunk, chunks):
    rows, width = query.shape
    heads = width // HD
    groups = heads // HG
    per = groups // chunks
    base = chunk * per
    cw = HG * HD
    part = per * cw
    nbd = rows // BS
    span = (5 + R) * BS
    g = 5 * BS
    hc = per * HG

    def tile(j, col):
        return pl.BlockSpec((BS, cw), lambda n, h, s: (n + j, h + col))

    def rand_tile(j, col):
        return pl.BlockSpec((1, BS, cw), lambda n, h, s: (s[n * R + j], 0, h + col))

    row_spec = pl.BlockSpec((BS, cw), lambda n, h, s: (n, h + base))
    in_specs = (
        [row_spec, row_spec, pl.BlockSpec((1, 1, span), lambda n, h, s: (n, 0, 0))]
        + [tile(j, base) for j in range(3)]
        + [tile(j, groups + base) for j in range(3)]
        + [
            pl.BlockSpec((2 * BS, cw), lambda n, h, s: (0, h + base)),
            pl.BlockSpec((2 * BS, cw), lambda n, h, s: (0, h + groups + base)),
        ]
        + [rand_tile(j, 0) for j in range(R)]
        + [rand_tile(j, per) for j in range(R)]
    )
    own_row = pl.BlockSpec((BS, cw), lambda n, h, s: (n, h))
    rand_spec = pl.BlockSpec((1, R * BS, cw), lambda n, h, s: (n, 0, h))
    prob_spec = pl.BlockSpec((1, HG, BS, g), lambda n, h, s: (n, h, 0, 0))
    out_specs = [own_row, own_row, rand_spec, rand_spec, prob_spec, prob_spec]
    out_shape = [
        jax.ShapeDtypeStruct((rows, part), jnp.bfloat16),
        jax.ShapeDtypeStruct((rows, part), jnp.bfloat16),
        jax.ShapeDtypeStruct((nbd, R * BS, part), jnp.bfloat16),
        jax.ShapeDtypeStruct((nbd, R * BS, part), jnp.bfloat16),
        jax.ShapeDtypeStruct((nbd, hc, BS, g), jnp.bfloat16),
        jax.ShapeDtypeStruct((nbd, hc, BS, g), jnp.bfloat16),
    ]
    grid_spec = pltpu.PrefetchScalarGridSpec(
        num_scalar_prefetch=1,
        grid=(nbd, per),
        in_specs=in_specs,
        out_specs=out_specs,
    )
    args = [query, dout, mask] + [padded] * 6 + [glob] * 2 + [fetched] * (2 * R)
    out, dq, rk, rv, pb, dsb = pl.pallas_call(
        scores_kernel,
        grid_spec=grid_spec,
        out_shape=out_shape,
        interpret=INTERPRET,
    )(slots, *args)

    row2 = pl.BlockSpec((BS, cw), lambda n, h: (n, h + base))
    prob2 = pl.BlockSpec((1, HG, BS, g), lambda n, h: (n, h, 0, 0))

    def term_spec(size):
        return pl.BlockSpec((1, size, cw), lambda n, h: (n, 0, h))

    wk, wv, gk, gv = pl.pallas_call(
        terms_kernel,
        grid=(nbd, per),
        in_specs=[row2, row2, prob2, prob2],
        out_specs=[term_spec(3 * BS), term_spec(3 * BS), term_spec(2 * BS), term_spec(2 * BS)],
        out_shape=[
            jax.ShapeDtypeStruct((nbd, 3 * BS, part), jnp.float32),
            jax.ShapeDtypeStruct((nbd, 3 * BS, part), jnp.float32),
            jax.ShapeDtypeStruct((nbd, 2 * BS, part), jnp.float32),
            jax.ShapeDtypeStruct((nbd, 2 * BS, part), jnp.float32),
        ],
        interpret=INTERPRET,
    )(query, dout, pb, dsb)
    return out, dq, wk, wv, gk, gv, rk, rv


def overlap(terms, nbd):
    width = terms.shape[-1]
    w4 = terms.reshape(nbd, 3, BS, width)
    return (
        jnp.pad(w4[:, 0], ((0, 2), (0, 0), (0, 0)))
        + jnp.pad(w4[:, 1], ((1, 1), (0, 0), (0, 0)))
        + jnp.pad(w4[:, 2], ((2, 0), (0, 0), (0, 0)))
    )


def body(query, key, value, dout, rand):
    rows, width = query.shape
    ndev = lax.axis_size(("head", "blk"))
    me = lax.axis_index(("head", "blk"))
    nbd = rows // BS
    total = nbd * ndev
    cap = (R * nbd + ndev - 1) // ndev
    pf = jnp.float32
    span = (5 + R) * BS
    pair = jnp.concatenate([key, value], axis=1)
    padded = extended(pair, ((("head", "blk"), 0),), BS)
    glob = from_root(pair[: 2 * BS], ("head", "blk"), 0)
    flat = rand.reshape(ndev, nbd * R)
    owner = flat // nbd
    local = flat - owner * nbd
    hit = owner == me
    order = jnp.cumsum(hit.astype(jnp.int32), axis=1) - 1
    slot_ids = jnp.arange(cap, dtype=jnp.int32)
    chosen = hit[:, None, :] & (order[:, None, :] == slot_ids[None, :, None])
    block_id = jnp.sum(jnp.where(chosen, local[:, None, :], 0), axis=2).reshape(-1)
    filled = jnp.any(chosen, axis=2).reshape(-1)
    tiles = pair.reshape(nbd, BS, 2 * width)
    outgoing = jnp.where(
        filled[:, None, None], jnp.take(tiles, block_id, axis=0), jnp.zeros((), pair.dtype)
    )
    mine = lax.dynamic_slice_in_dim(rand, me * nbd, nbd, 0).reshape(-1)
    mine_owner = mine // nbd
    count = mine.shape[0]
    earlier = jnp.arange(count)[:, None] > jnp.arange(count)[None, :]
    same = mine_owner[:, None] == mine_owner[None, :]
    mine_rank = jnp.sum(earlier & same, axis=1)
    mine_slot = (mine_owner * cap + mine_rank).astype(jnp.int32)
    first = me * nbd + jnp.arange(nbd, dtype=jnp.int32)
    always = first >= 0
    valid = jnp.concatenate(
        [
            jnp.stack([first > 0, always, first < total - 1, always, always], axis=1),
            jnp.ones((nbd, R), bool),
        ],
        axis=1,
    )
    mask = jnp.repeat(valid, BS, axis=1).astype(pf).reshape(nbd, 1, span)
    match = mine_slot[None, :] == jnp.arange(ndev * cap, dtype=jnp.int32)[:, None]
    source = jnp.argmax(match, axis=1)
    present = jnp.any(match, axis=1)[:, None, None]
    onehot = (
        (block_id[None, :] == jnp.arange(nbd, dtype=jnp.int32)[:, None]) & filled[None, :]
    ).astype(jnp.bfloat16)
    chunks = CHUNKS
    part = width // chunks
    results = []
    previous = None
    for c in range(chunks):
        cols = jnp.concatenate(
            [outgoing[..., c * part : (c + 1) * part], outgoing[..., width + c * part : width + (c + 1) * part]],
            axis=-1,
        )
        if previous is None:
            cols, _, _ = lax.optimization_barrier((cols, padded, glob))
        else:
            cols, _ = lax.optimization_barrier((cols, previous))
        fetched = lax.all_to_all(cols, ("head", "blk"), split_axis=0, concat_axis=0, tiled=True)
        previous = fetched
        out, dq, wk, wv, gk, gv, rk, rv = attention(
            query, dout, mask, padded, glob, fetched, mine_slot, c, chunks
        )
        sk = overlap(wk, nbd)
        sv = overlap(wv, nbd)
        rims = jnp.concatenate(
            [
                jnp.concatenate([sk[0], sv[0]], axis=-1),
                jnp.concatenate([sk[nbd + 1], sv[nbd + 1]], axis=-1),
            ],
            axis=0,
        )
        arrived = extended(rims.astype(jnp.bfloat16), ((("head", "blk"), 0),), BS).astype(pf)
        own = jnp.concatenate([sk[1 : nbd + 1], sv[1 : nbd + 1]], axis=-1)
        glob_grad = jnp.concatenate([jnp.sum(gk, axis=0), jnp.sum(gv, axis=0)], axis=-1).reshape(
            2, BS, 2 * part
        )
        glob_total = lax.psum(glob_grad.astype(jnp.bfloat16), ("head", "blk")).astype(pf)
        edge = jnp.concatenate(
            [arrived[None, :BS], jnp.zeros((nbd - 2, BS, 2 * part), pf), arrived[None, 3 * BS :]], axis=0
        )
        lead = jnp.pad(jnp.where(me == 0, glob_total, 0.0), ((0, nbd - 2), (0, 0), (0, 0)))
        own = own + edge + lead
        rand_grad = jnp.concatenate([rk, rv], axis=-1).reshape(nbd * R, BS, 2 * part)
        returning = jnp.where(present, jnp.take(rand_grad, source, axis=0), jnp.zeros((), jnp.bfloat16))
        back = lax.all_to_all(returning, ("head", "blk"), split_axis=0, concat_axis=0, tiled=True)
        own = own + jnp.dot(
            onehot, back.reshape(ndev * cap, BS * 2 * part), preferred_element_type=pf
        ).reshape(nbd, BS, 2 * part)
        dk = own[..., :part].astype(jnp.bfloat16).reshape(rows, part)
        dv = own[..., part:].astype(jnp.bfloat16).reshape(rows, part)
        results.append((out, dq, dk, dv))
    return tuple(jnp.concatenate([r[i] for r in results], axis=1) for i in range(4))


def solution(mesh):
    placed = (
        P(("dp", "head", "blk"), None),
        P(("dp", "head", "blk"), None),
        P(("dp", "head", "blk"), None),
        P(("dp", "head", "blk"), None),
        P("dp", None),
    )
    return jax.shard_map(
        body,
        mesh=mesh,
        in_specs=placed,
        out_specs=(
            P(("dp", "head", "blk"), None),
            P(("dp", "head", "blk"), None),
            P(("dp", "head", "blk"), None),
            P(("dp", "head", "blk"), None),
        ),
        check_vma=False,
    )
```

```python
import math

import jax
import jax.numpy as jnp
from jax import lax
from jax.experimental import pallas as pl
from jax.experimental.pallas import tpu as pltpu
from jax.sharding import PartitionSpec as P

HD = 128
BS = 64
R = 3


NEG = -1e30
INTERPRET = False
HG = 4


def extended(block, sides, width):
    for axis, dim in sides:
        count = lax.axis_size(axis)
        forward = [(i, i + 1) for i in range(count - 1)]
        backward = [(target, source) for source, target in forward]
        low = lax.ppermute(
            lax.slice_in_dim(block, block.shape[dim] - width, None, axis=dim), axis, forward
        )
        high = lax.ppermute(lax.slice_in_dim(block, 0, width, axis=dim), axis, backward)
        block = jnp.concatenate([low, block, high], axis=dim)
    return block


def spread(pieces, axis):
    return lax.all_to_all(pieces, axis, split_axis=0, concat_axis=0, tiled=True)


def from_root(value, axis):
    n = lax.axis_size(axis)
    pieces = value.reshape(n, -1)
    mine = spread(pieces, axis)[0]
    return spread(jnp.broadcast_to(mine[None], pieces.shape), axis).reshape(value.shape)


def sum_all(value, axis):
    n = lax.axis_size(axis)
    pieces = value.reshape(n, -1)
    mine = jnp.sum(spread(pieces, axis).astype(jnp.float32), axis=0).astype(value.dtype)
    return spread(jnp.broadcast_to(mine[None], pieces.shape), axis).reshape(value.shape)


def scores_kernel(
    slots_ref, q_ref, do_ref, mask_ref,
    kw0, kw1, kw2, vw0, vw1, vw2, kg, vg, kr0, kr1, kr2, vr0, vr1, vr2,
    out_ref, dq_ref, rk_ref, rv_ref, pb_ref, dsb_ref,
):
    pf = jnp.float32
    scale = 1.0 / math.sqrt(HD)
    nt = (((1,), (1,)), ((), ()))
    tn = (((0,), (0,)), ((), ()))
    g = 5 * BS
    valid = mask_ref[0] > 0
    for t in range(HG):
        c = slice(t * HD, (t + 1) * HD)
        q = q_ref[:, c]
        do = do_ref[:, c]
        k = jnp.concatenate(
            [kw0[:, c], kw1[:, c], kw2[:, c], kg[:, c], kr0[0, :, c], kr1[0, :, c], kr2[0, :, c]], axis=0
        )
        v = jnp.concatenate(
            [vw0[:, c], vw1[:, c], vw2[:, c], vg[:, c], vr0[0, :, c], vr1[0, :, c], vr2[0, :, c]], axis=0
        )
        s = lax.dot_general(q, k, nt, preferred_element_type=pf) * scale
        s = jnp.where(valid, s, NEG)
        top = jnp.max(s, axis=1, keepdims=True)
        e = jnp.exp(s - top)
        p = e / jnp.sum(e, axis=1, keepdims=True)
        pb = p.astype(jnp.bfloat16)
        ob = jnp.dot(pb, v, preferred_element_type=pf).astype(jnp.bfloat16)
        out_ref[:, c] = ob
        delta = jnp.sum(do.astype(pf) * ob.astype(pf), axis=1, keepdims=True)
        dp = lax.dot_general(do, v, nt, preferred_element_type=pf)
        ds = p * (dp - delta)
        dsb = ds.astype(jnp.bfloat16)
        dq_ref[:, c] = (jnp.dot(dsb, k, preferred_element_type=pf) * scale).astype(jnp.bfloat16)
        rk_ref[0, :, c] = (
            lax.dot_general(dsb[:, g:], q, tn, preferred_element_type=pf) * scale
        ).astype(jnp.bfloat16)
        rv_ref[0, :, c] = lax.dot_general(pb[:, g:], do, tn, preferred_element_type=pf).astype(jnp.bfloat16)
        pb_ref[0, t] = pb[:, :g]
        dsb_ref[0, t] = dsb[:, :g]


def terms_kernel(q_ref, do_ref, pb_ref, dsb_ref, wk_ref, wv_ref, gk_ref, gv_ref):
    pf = jnp.float32
    scale = 1.0 / math.sqrt(HD)
    tn = (((0,), (0,)), ((), ()))
    w = 3 * BS
    for t in range(HG):
        c = slice(t * HD, (t + 1) * HD)
        kt = lax.dot_general(dsb_ref[0, t], q_ref[:, c], tn, preferred_element_type=pf) * scale
        vt = lax.dot_general(pb_ref[0, t], do_ref[:, c], tn, preferred_element_type=pf)
        wk_ref[0, :, c] = kt[:w]
        wv_ref[0, :, c] = vt[:w]
        gk_ref[0, :, c] = kt[w:]
        gv_ref[0, :, c] = vt[w:]


def attention(query, dout, mask, padded, glob, fetched, slots):
    rows, width = query.shape
    heads = width // HD
    groups = heads // HG
    cw = HG * HD
    nbd = rows // BS
    span = (5 + R) * BS
    g = 5 * BS

    def tile(j, col):
        return pl.BlockSpec((BS, cw), lambda n, h, s: (n + j, h + col))

    def rand_tile(j, col):
        return pl.BlockSpec((1, BS, cw), lambda n, h, s: (s[n * R + j], 0, h + col))

    row_spec = pl.BlockSpec((BS, cw), lambda n, h, s: (n, h))
    in_specs = (
        [row_spec, row_spec, pl.BlockSpec((1, 1, span), lambda n, h, s: (n, 0, 0))]
        + [tile(j, 0) for j in range(3)]
        + [tile(j, groups) for j in range(3)]
        + [
            pl.BlockSpec((2 * BS, cw), lambda n, h, s: (0, h)),
            pl.BlockSpec((2 * BS, cw), lambda n, h, s: (0, h + groups)),
        ]
        + [rand_tile(j, 0) for j in range(R)]
        + [rand_tile(j, groups) for j in range(R)]
    )
    rand_spec = pl.BlockSpec((1, R * BS, cw), lambda n, h, s: (n, 0, h))
    prob_spec = pl.BlockSpec((1, HG, BS, g), lambda n, h, s: (n, h, 0, 0))
    out_specs = [row_spec, row_spec, rand_spec, rand_spec, prob_spec, prob_spec]
    out_shape = [
        jax.ShapeDtypeStruct((rows, width), jnp.bfloat16),
        jax.ShapeDtypeStruct((rows, width), jnp.bfloat16),
        jax.ShapeDtypeStruct((nbd, R * BS, width), jnp.bfloat16),
        jax.ShapeDtypeStruct((nbd, R * BS, width), jnp.bfloat16),
        jax.ShapeDtypeStruct((nbd, heads, BS, g), jnp.bfloat16),
        jax.ShapeDtypeStruct((nbd, heads, BS, g), jnp.bfloat16),
    ]
    grid_spec = pltpu.PrefetchScalarGridSpec(
        num_scalar_prefetch=1,
        grid=(nbd, groups),
        in_specs=in_specs,
        out_specs=out_specs,
    )
    args = [query, dout, mask] + [padded] * 6 + [glob] * 2 + [fetched] * (2 * R)
    out, dq, rk, rv, pb, dsb = pl.pallas_call(
        scores_kernel,
        grid_spec=grid_spec,
        out_shape=out_shape,
        interpret=INTERPRET,
    )(slots, *args)

    row2 = pl.BlockSpec((BS, cw), lambda n, h: (n, h))
    prob2 = pl.BlockSpec((1, HG, BS, g), lambda n, h: (n, h, 0, 0))

    def term_spec(size):
        return pl.BlockSpec((1, size, cw), lambda n, h: (n, 0, h))

    wk, wv, gk, gv = pl.pallas_call(
        terms_kernel,
        grid=(nbd, groups),
        in_specs=[row2, row2, prob2, prob2],
        out_specs=[term_spec(3 * BS), term_spec(3 * BS), term_spec(2 * BS), term_spec(2 * BS)],
        out_shape=[
            jax.ShapeDtypeStruct((nbd, 3 * BS, width), jnp.float32),
            jax.ShapeDtypeStruct((nbd, 3 * BS, width), jnp.float32),
            jax.ShapeDtypeStruct((nbd, 2 * BS, width), jnp.float32),
            jax.ShapeDtypeStruct((nbd, 2 * BS, width), jnp.float32),
        ],
        interpret=INTERPRET,
    )(query, dout, pb, dsb)
    return out, dq, wk, wv, gk, gv, rk, rv


def overlap(terms, nbd):
    width = terms.shape[-1]
    w4 = terms.reshape(nbd, 3, BS, width)
    return (
        jnp.pad(w4[:, 0], ((0, 2), (0, 0), (0, 0)))
        + jnp.pad(w4[:, 1], ((1, 1), (0, 0), (0, 0)))
        + jnp.pad(w4[:, 2], ((2, 0), (0, 0), (0, 0)))
    )


def body(query, key, value, dout, rand):
    rows, width = query.shape
    ndev = lax.axis_size(("head", "blk"))
    me = lax.axis_index(("head", "blk"))
    nbd = rows // BS
    total = nbd * ndev
    cap = (R * nbd + ndev - 1) // ndev
    pf = jnp.float32
    span = (5 + R) * BS
    pair = jnp.concatenate([key, value], axis=1)
    padded = extended(pair, ((("head", "blk"), 0),), BS)
    glob = from_root(pair[: 2 * BS], ("head", "blk"))
    flat = rand.reshape(ndev, nbd * R)
    owner = flat // nbd
    local = flat - owner * nbd
    hit = owner == me
    order = jnp.cumsum(hit.astype(jnp.int32), axis=1) - 1
    slot_ids = jnp.arange(cap, dtype=jnp.int32)
    chosen = hit[:, None, :] & (order[:, None, :] == slot_ids[None, :, None])
    block_id = jnp.sum(jnp.where(chosen, local[:, None, :], 0), axis=2).reshape(-1)
    filled = jnp.any(chosen, axis=2).reshape(-1)
    tiles = pair.reshape(nbd, BS, 2 * width)
    outgoing = jnp.where(
        filled[:, None, None], jnp.take(tiles, block_id, axis=0), jnp.zeros((), pair.dtype)
    )
    fetched = lax.all_to_all(outgoing, ("head", "blk"), split_axis=0, concat_axis=0, tiled=True)
    mine = lax.dynamic_slice_in_dim(rand, me * nbd, nbd, 0).reshape(-1)
    mine_owner = mine // nbd
    count = mine.shape[0]
    earlier = jnp.arange(count)[:, None] > jnp.arange(count)[None, :]
    same = mine_owner[:, None] == mine_owner[None, :]
    mine_rank = jnp.sum(earlier & same, axis=1)
    mine_slot = (mine_owner * cap + mine_rank).astype(jnp.int32)
    first = me * nbd + jnp.arange(nbd, dtype=jnp.int32)
    always = first >= 0
    valid = jnp.concatenate(
        [
            jnp.stack([first > 0, always, first < total - 1, always, always], axis=1),
            jnp.ones((nbd, R), bool),
        ],
        axis=1,
    )
    mask = jnp.repeat(valid, BS, axis=1).astype(pf).reshape(nbd, 1, span)
    out, dq, wk, wv, gk, gv, rk, rv = attention(query, dout, mask, padded, glob, fetched, mine_slot)
    sk = overlap(wk, nbd)
    sv = overlap(wv, nbd)
    rims = jnp.concatenate(
        [
            jnp.concatenate([sk[0], sv[0]], axis=-1),
            jnp.concatenate([sk[nbd + 1], sv[nbd + 1]], axis=-1),
        ],
        axis=0,
    )
    arrived = extended(rims.astype(jnp.bfloat16), ((("head", "blk"), 0),), BS).astype(pf)
    own = jnp.concatenate([sk[1 : nbd + 1], sv[1 : nbd + 1]], axis=-1)
    glob_grad = jnp.concatenate([jnp.sum(gk, axis=0), jnp.sum(gv, axis=0)], axis=-1).reshape(
        2, BS, 2 * width
    )
    glob_total = sum_all(glob_grad.astype(jnp.bfloat16), ("head", "blk")).astype(pf)
    edge = jnp.concatenate(
        [arrived[None, :BS], jnp.zeros((nbd - 2, BS, 2 * width), pf), arrived[None, 3 * BS :]], axis=0
    )
    lead = jnp.pad(jnp.where(me == 0, glob_total, 0.0), ((0, nbd - 2), (0, 0), (0, 0)))
    own = own + edge + lead
    rand_grad = jnp.concatenate([rk, rv], axis=-1).reshape(nbd * R, BS, 2 * width)
    match = mine_slot[None, :] == jnp.arange(ndev * cap, dtype=jnp.int32)[:, None]
    source = jnp.argmax(match, axis=1)
    returning = jnp.where(
        jnp.any(match, axis=1)[:, None, None],
        jnp.take(rand_grad, source, axis=0),
        jnp.zeros((), jnp.bfloat16),
    )
    back = lax.all_to_all(returning, ("head", "blk"), split_axis=0, concat_axis=0, tiled=True)
    onehot = (
        (block_id[None, :] == jnp.arange(nbd, dtype=jnp.int32)[:, None]) & filled[None, :]
    ).astype(jnp.bfloat16)
    own = own + jnp.dot(
        onehot, back.reshape(ndev * cap, BS * 2 * width), preferred_element_type=pf
    ).reshape(nbd, BS, 2 * width)
    dk = own[..., :width].astype(jnp.bfloat16).reshape(rows, width)
    dv = own[..., width:].astype(jnp.bfloat16).reshape(rows, width)
    return (out, dq, dk, dv)


def solution(mesh):
    placed = (
        P(("dp", "head", "blk"), None),
        P(("dp", "head", "blk"), None),
        P(("dp", "head", "blk"), None),
        P(("dp", "head", "blk"), None),
        P("dp", None),
    )
    return jax.shard_map(
        body,
        mesh=mesh,
        in_specs=placed,
        out_specs=(
            P(("dp", "head", "blk"), None),
            P(("dp", "head", "blk"), None),
            P(("dp", "head", "blk"), None),
            P(("dp", "head", "blk"), None),
        ),
        check_vma=False,
    )
```

```python
import math

import jax
import jax.numpy as jnp
from jax import lax
from jax.experimental import pallas as pl
from jax.experimental.pallas import tpu as pltpu
from jax.sharding import PartitionSpec as P

HD = 128
BS = 64
R = 3


NEG = -1e30
INTERPRET = False
HG = 4


def extended(block, sides, width):
    for axis, dim in sides:
        count = lax.axis_size(axis)
        forward = [(i, i + 1) for i in range(count - 1)]
        backward = [(target, source) for source, target in forward]
        low = lax.ppermute(
            lax.slice_in_dim(block, block.shape[dim] - width, None, axis=dim), axis, forward
        )
        high = lax.ppermute(lax.slice_in_dim(block, 0, width, axis=dim), axis, backward)
        block = jnp.concatenate([low, block, high], axis=dim)
    return block


def spread(pieces, axis):
    return lax.all_to_all(pieces, axis, split_axis=0, concat_axis=0, tiled=True)


def from_root(value, axis):
    n = lax.axis_size(axis)
    pieces = value.reshape(n, -1)
    mine = spread(pieces, axis)[0]
    return spread(jnp.broadcast_to(mine[None], pieces.shape), axis).reshape(value.shape)


def sum_all(value, axis):
    n = lax.axis_size(axis)
    pieces = value.reshape(n, -1)
    mine = jnp.sum(spread(pieces, axis).astype(jnp.float32), axis=0).astype(value.dtype)
    return spread(jnp.broadcast_to(mine[None], pieces.shape), axis).reshape(value.shape)


def scores_kernel(
    slots_ref, q_ref, do_ref, mask_ref,
    kw0, kw1, kw2, vw0, vw1, vw2, kg, vg, kr0, kr1, kr2, vr0, vr1, vr2,
    out_ref, dq_ref, rk_ref, rv_ref, pb_ref, dsb_ref,
):
    pf = jnp.float32
    scale = 1.0 / math.sqrt(HD)
    nt = (((1,), (1,)), ((), ()))
    tn = (((0,), (0,)), ((), ()))
    g = 5 * BS
    valid = mask_ref[0] > 0
    for t in range(HG):
        c = slice(t * HD, (t + 1) * HD)
        q = q_ref[:, c]
        do = do_ref[:, c]
        k = jnp.concatenate(
            [kw0[:, c], kw1[:, c], kw2[:, c], kg[:, c], kr0[0, :, c], kr1[0, :, c], kr2[0, :, c]], axis=0
        )
        v = jnp.concatenate(
            [vw0[:, c], vw1[:, c], vw2[:, c], vg[:, c], vr0[0, :, c], vr1[0, :, c], vr2[0, :, c]], axis=0
        )
        s = lax.dot_general(q, k, nt, preferred_element_type=pf) * scale
        s = jnp.where(valid, s, NEG)
        top = jnp.max(s, axis=1, keepdims=True)
        e = jnp.exp(s - top)
        p = e / jnp.sum(e, axis=1, keepdims=True)
        pb = p.astype(jnp.bfloat16)
        ob = jnp.dot(pb, v, preferred_element_type=pf).astype(jnp.bfloat16)
        out_ref[:, c] = ob
        delta = jnp.sum(do.astype(pf) * ob.astype(pf), axis=1, keepdims=True)
        dp = lax.dot_general(do, v, nt, preferred_element_type=pf)
        ds = p * (dp - delta)
        dsb = ds.astype(jnp.bfloat16)
        dq_ref[:, c] = (jnp.dot(dsb, k, preferred_element_type=pf) * scale).astype(jnp.bfloat16)
        rk_ref[0, :, c] = (
            lax.dot_general(dsb[:, g:], q, tn, preferred_element_type=pf) * scale
        ).astype(jnp.bfloat16)
        rv_ref[0, :, c] = lax.dot_general(pb[:, g:], do, tn, preferred_element_type=pf).astype(jnp.bfloat16)
        pb_ref[0, t] = pb[:, :g]
        dsb_ref[0, t] = dsb[:, :g]


def terms_kernel(q_ref, do_ref, pb_ref, dsb_ref, wk_ref, wv_ref, gk_ref, gv_ref):
    pf = jnp.float32
    scale = 1.0 / math.sqrt(HD)
    tn = (((0,), (0,)), ((), ()))
    w = 3 * BS
    for t in range(HG):
        c = slice(t * HD, (t + 1) * HD)
        kt = lax.dot_general(dsb_ref[0, t], q_ref[:, c], tn, preferred_element_type=pf) * scale
        vt = lax.dot_general(pb_ref[0, t], do_ref[:, c], tn, preferred_element_type=pf)
        wk_ref[0, :, c] = kt[:w]
        wv_ref[0, :, c] = vt[:w]
        gk_ref[0, :, c] = kt[w:]
        gv_ref[0, :, c] = vt[w:]


def attention(query, dout, mask, padded, glob, fetched, slots):
    rows, width = query.shape
    heads = width // HD
    groups = heads // HG
    cw = HG * HD
    nbd = rows // BS
    span = (5 + R) * BS
    g = 5 * BS

    def tile(j, col):
        return pl.BlockSpec((BS, cw), lambda n, h, s: (n + j, h + col))

    def rand_tile(j, col):
        return pl.BlockSpec((1, BS, cw), lambda n, h, s: (s[n * R + j], 0, h + col))

    row_spec = pl.BlockSpec((BS, cw), lambda n, h, s: (n, h))
    in_specs = (
        [row_spec, row_spec, pl.BlockSpec((1, 1, span), lambda n, h, s: (n, 0, 0))]
        + [tile(j, 0) for j in range(3)]
        + [tile(j, groups) for j in range(3)]
        + [
            pl.BlockSpec((2 * BS, cw), lambda n, h, s: (0, h)),
            pl.BlockSpec((2 * BS, cw), lambda n, h, s: (0, h + groups)),
        ]
        + [rand_tile(j, 0) for j in range(R)]
        + [rand_tile(j, groups) for j in range(R)]
    )
    rand_spec = pl.BlockSpec((1, R * BS, cw), lambda n, h, s: (n, 0, h))
    prob_spec = pl.BlockSpec((1, HG, BS, g), lambda n, h, s: (n, h, 0, 0))
    out_specs = [row_spec, row_spec, rand_spec, rand_spec, prob_spec, prob_spec]
    out_shape = [
        jax.ShapeDtypeStruct((rows, width), jnp.bfloat16),
        jax.ShapeDtypeStruct((rows, width), jnp.bfloat16),
        jax.ShapeDtypeStruct((nbd, R * BS, width), jnp.bfloat16),
        jax.ShapeDtypeStruct((nbd, R * BS, width), jnp.bfloat16),
        jax.ShapeDtypeStruct((nbd, heads, BS, g), jnp.bfloat16),
        jax.ShapeDtypeStruct((nbd, heads, BS, g), jnp.bfloat16),
    ]
    grid_spec = pltpu.PrefetchScalarGridSpec(
        num_scalar_prefetch=1,
        grid=(nbd, groups),
        in_specs=in_specs,
        out_specs=out_specs,
    )
    args = [query, dout, mask] + [padded] * 6 + [glob] * 2 + [fetched] * (2 * R)
    out, dq, rk, rv, pb, dsb = pl.pallas_call(
        scores_kernel,
        grid_spec=grid_spec,
        out_shape=out_shape,
        interpret=INTERPRET,
    )(slots, *args)

    return out, dq, rk, rv, pb, dsb


def window_terms(query, dout, pb, dsb):
    rows, width = query.shape
    heads = width // HD
    groups = heads // HG
    cw = HG * HD
    nbd = rows // BS
    g = 5 * BS
    row2 = pl.BlockSpec((BS, cw), lambda n, h: (n, h))
    prob2 = pl.BlockSpec((1, HG, BS, g), lambda n, h: (n, h, 0, 0))

    def term_spec(size):
        return pl.BlockSpec((1, size, cw), lambda n, h: (n, 0, h))

    return pl.pallas_call(
        terms_kernel,
        grid=(nbd, groups),
        in_specs=[row2, row2, prob2, prob2],
        out_specs=[term_spec(3 * BS), term_spec(3 * BS), term_spec(2 * BS), term_spec(2 * BS)],
        out_shape=[
            jax.ShapeDtypeStruct((nbd, 3 * BS, width), jnp.float32),
            jax.ShapeDtypeStruct((nbd, 3 * BS, width), jnp.float32),
            jax.ShapeDtypeStruct((nbd, 2 * BS, width), jnp.float32),
            jax.ShapeDtypeStruct((nbd, 2 * BS, width), jnp.float32),
        ],
        interpret=INTERPRET,
    )(query, dout, pb, dsb)


def overlap(terms, nbd):
    width = terms.shape[-1]
    w4 = terms.reshape(nbd, 3, BS, width)
    return (
        jnp.pad(w4[:, 0], ((0, 2), (0, 0), (0, 0)))
        + jnp.pad(w4[:, 1], ((1, 1), (0, 0), (0, 0)))
        + jnp.pad(w4[:, 2], ((2, 0), (0, 0), (0, 0)))
    )


def body(query, key, value, dout, rand):
    rows, width = query.shape
    ndev = lax.axis_size(("head", "blk"))
    me = lax.axis_index(("head", "blk"))
    nbd = rows // BS
    total = nbd * ndev
    cap = (R * nbd + ndev - 1) // ndev
    pf = jnp.float32
    span = (5 + R) * BS
    pair = jnp.concatenate([key, value], axis=1)
    padded = extended(pair, ((("head", "blk"), 0),), BS)
    glob = from_root(pair[: 2 * BS], ("head", "blk"))
    flat = rand.reshape(ndev, nbd * R)
    owner = flat // nbd
    local = flat - owner * nbd
    hit = owner == me
    order = jnp.cumsum(hit.astype(jnp.int32), axis=1) - 1
    slot_ids = jnp.arange(cap, dtype=jnp.int32)
    chosen = hit[:, None, :] & (order[:, None, :] == slot_ids[None, :, None])
    block_id = jnp.sum(jnp.where(chosen, local[:, None, :], 0), axis=2).reshape(-1)
    filled = jnp.any(chosen, axis=2).reshape(-1)
    tiles = pair.reshape(nbd, BS, 2 * width)
    outgoing = jnp.where(
        filled[:, None, None], jnp.take(tiles, block_id, axis=0), jnp.zeros((), pair.dtype)
    )
    fetched = lax.all_to_all(outgoing, ("head", "blk"), split_axis=0, concat_axis=0, tiled=True)
    mine = lax.dynamic_slice_in_dim(rand, me * nbd, nbd, 0).reshape(-1)
    mine_owner = mine // nbd
    count = mine.shape[0]
    earlier = jnp.arange(count)[:, None] > jnp.arange(count)[None, :]
    same = mine_owner[:, None] == mine_owner[None, :]
    mine_rank = jnp.sum(earlier & same, axis=1)
    mine_slot = (mine_owner * cap + mine_rank).astype(jnp.int32)
    first = me * nbd + jnp.arange(nbd, dtype=jnp.int32)
    always = first >= 0
    valid = jnp.concatenate(
        [
            jnp.stack([first > 0, always, first < total - 1, always, always], axis=1),
            jnp.ones((nbd, R), bool),
        ],
        axis=1,
    )
    mask = jnp.repeat(valid, BS, axis=1).astype(pf).reshape(nbd, 1, span)
    out, dq, rk, rv, pb, dsb = attention(query, dout, mask, padded, glob, fetched, mine_slot)
    rand_grad = jnp.concatenate([rk, rv], axis=-1).reshape(nbd * R, BS, 2 * width)
    match = mine_slot[None, :] == jnp.arange(ndev * cap, dtype=jnp.int32)[:, None]
    source = jnp.argmax(match, axis=1)
    returning = jnp.where(
        jnp.any(match, axis=1)[:, None, None],
        jnp.take(rand_grad, source, axis=0),
        jnp.zeros((), jnp.bfloat16),
    )
    back = lax.all_to_all(returning, ("head", "blk"), split_axis=0, concat_axis=0, tiled=True)
    pb, dsb, _ = lax.optimization_barrier((pb, dsb, returning))
    wk, wv, gk, gv = window_terms(query, dout, pb, dsb)
    sk = overlap(wk, nbd)
    sv = overlap(wv, nbd)
    rims = jnp.concatenate(
        [
            jnp.concatenate([sk[0], sv[0]], axis=-1),
            jnp.concatenate([sk[nbd + 1], sv[nbd + 1]], axis=-1),
        ],
        axis=0,
    )
    arrived = extended(rims.astype(jnp.bfloat16), ((("head", "blk"), 0),), BS).astype(pf)
    own = jnp.concatenate([sk[1 : nbd + 1], sv[1 : nbd + 1]], axis=-1)
    glob_grad = jnp.concatenate([jnp.sum(gk, axis=0), jnp.sum(gv, axis=0)], axis=-1).reshape(
        2, BS, 2 * width
    )
    glob_grad, _ = lax.optimization_barrier((glob_grad, back))
    glob_total = sum_all(glob_grad.astype(jnp.bfloat16), ("head", "blk")).astype(pf)
    edge = jnp.concatenate(
        [arrived[None, :BS], jnp.zeros((nbd - 2, BS, 2 * width), pf), arrived[None, 3 * BS :]], axis=0
    )
    lead = jnp.pad(jnp.where(me == 0, glob_total, 0.0), ((0, nbd - 2), (0, 0), (0, 0)))
    own = own + edge + lead
    onehot = (
        (block_id[None, :] == jnp.arange(nbd, dtype=jnp.int32)[:, None]) & filled[None, :]
    ).astype(jnp.bfloat16)
    own = own + jnp.dot(
        onehot, back.reshape(ndev * cap, BS * 2 * width), preferred_element_type=pf
    ).reshape(nbd, BS, 2 * width)
    dk = own[..., :width].astype(jnp.bfloat16).reshape(rows, width)
    dv = own[..., width:].astype(jnp.bfloat16).reshape(rows, width)
    return (out, dq, dk, dv)


def solution(mesh):
    placed = (
        P(("dp", "head", "blk"), None),
        P(("dp", "head", "blk"), None),
        P(("dp", "head", "blk"), None),
        P(("dp", "head", "blk"), None),
        P("dp", None),
    )
    return jax.shard_map(
        body,
        mesh=mesh,
        in_specs=placed,
        out_specs=(
            P(("dp", "head", "blk"), None),
            P(("dp", "head", "blk"), None),
            P(("dp", "head", "blk"), None),
            P(("dp", "head", "blk"), None),
        ),
        check_vma=False,
    )
```

```python
import math

import jax
import jax.numpy as jnp
from jax import lax
from jax.experimental import pallas as pl
from jax.experimental.pallas import tpu as pltpu
from jax.sharding import PartitionSpec as P

HD = 128
BS = 64
R = 3


NEG = -1e30
INTERPRET = False
HG = 4


def extended(block, sides, width):
    for axis, dim in sides:
        count = lax.axis_size(axis)
        forward = [(i, i + 1) for i in range(count - 1)]
        backward = [(target, source) for source, target in forward]
        low = lax.ppermute(
            lax.slice_in_dim(block, block.shape[dim] - width, None, axis=dim), axis, forward
        )
        high = lax.ppermute(lax.slice_in_dim(block, 0, width, axis=dim), axis, backward)
        block = jnp.concatenate([low, block, high], axis=dim)
    return block


def spread(pieces, axis):
    return lax.all_to_all(pieces, axis, split_axis=0, concat_axis=0, tiled=True)


def from_root(value, axis):
    n = lax.axis_size(axis)
    pieces = value.reshape(n, -1)
    mine = spread(pieces, axis)[0]
    return spread(jnp.broadcast_to(mine[None], pieces.shape), axis).reshape(value.shape)


def scores_kernel(
    slots_ref, q_ref, do_ref, mask_ref,
    kw0, kw1, kw2, vw0, vw1, vw2, kg, vg, kr0, kr1, kr2, vr0, vr1, vr2,
    out_ref, dq_ref, rk_ref, rv_ref, pb_ref, dsb_ref,
):
    pf = jnp.float32
    scale = 1.0 / math.sqrt(HD)
    nt = (((1,), (1,)), ((), ()))
    tn = (((0,), (0,)), ((), ()))
    g = 5 * BS
    valid = mask_ref[0] > 0
    for t in range(HG):
        c = slice(t * HD, (t + 1) * HD)
        q = q_ref[:, c]
        do = do_ref[:, c]
        k = jnp.concatenate(
            [kw0[:, c], kw1[:, c], kw2[:, c], kg[:, c], kr0[0, :, c], kr1[0, :, c], kr2[0, :, c]], axis=0
        )
        v = jnp.concatenate(
            [vw0[:, c], vw1[:, c], vw2[:, c], vg[:, c], vr0[0, :, c], vr1[0, :, c], vr2[0, :, c]], axis=0
        )
        s = lax.dot_general(q, k, nt, preferred_element_type=pf) * scale
        s = jnp.where(valid, s, NEG)
        top = jnp.max(s, axis=1, keepdims=True)
        e = jnp.exp(s - top)
        p = e / jnp.sum(e, axis=1, keepdims=True)
        pb = p.astype(jnp.bfloat16)
        ob = jnp.dot(pb, v, preferred_element_type=pf).astype(jnp.bfloat16)
        out_ref[:, c] = ob
        delta = jnp.sum(do.astype(pf) * ob.astype(pf), axis=1, keepdims=True)
        dp = lax.dot_general(do, v, nt, preferred_element_type=pf)
        ds = p * (dp - delta)
        dsb = ds.astype(jnp.bfloat16)
        dq_ref[:, c] = (jnp.dot(dsb, k, preferred_element_type=pf) * scale).astype(jnp.bfloat16)
        rk_ref[0, :, c] = (
            lax.dot_general(dsb[:, g:], q, tn, preferred_element_type=pf) * scale
        ).astype(jnp.bfloat16)
        rv_ref[0, :, c] = lax.dot_general(pb[:, g:], do, tn, preferred_element_type=pf).astype(jnp.bfloat16)
        pb_ref[0, t] = pb[:, :g]
        dsb_ref[0, t] = dsb[:, :g]


def terms_kernel(q_ref, do_ref, pb_ref, dsb_ref, wk_ref, wv_ref, gk_ref, gv_ref):
    pf = jnp.float32
    scale = 1.0 / math.sqrt(HD)
    tn = (((0,), (0,)), ((), ()))
    w = 3 * BS
    for t in range(HG):
        c = slice(t * HD, (t + 1) * HD)
        kt = lax.dot_general(dsb_ref[0, t], q_ref[:, c], tn, preferred_element_type=pf) * scale
        vt = lax.dot_general(pb_ref[0, t], do_ref[:, c], tn, preferred_element_type=pf)
        wk_ref[0, :, c] = kt[:w]
        wv_ref[0, :, c] = vt[:w]
        gk_ref[0, :, c] = kt[w:]
        gv_ref[0, :, c] = vt[w:]


def attention(query, dout, mask, padded, glob, fetched, slots):
    rows, width = query.shape
    heads = width // HD
    groups = heads // HG
    cw = HG * HD
    nbd = rows // BS
    span = (5 + R) * BS
    g = 5 * BS

    def tile(j, col):
        return pl.BlockSpec((BS, cw), lambda n, h, s: (n + j, h + col))

    def rand_tile(j, col):
        return pl.BlockSpec((1, BS, cw), lambda n, h, s: (s[n * R + j], 0, h + col))

    row_spec = pl.BlockSpec((BS, cw), lambda n, h, s: (n, h))
    in_specs = (
        [row_spec, row_spec, pl.BlockSpec((1, 1, span), lambda n, h, s: (n, 0, 0))]
        + [tile(j, 0) for j in range(3)]
        + [tile(j, groups) for j in range(3)]
        + [
            pl.BlockSpec((2 * BS, cw), lambda n, h, s: (0, h)),
            pl.BlockSpec((2 * BS, cw), lambda n, h, s: (0, h + groups)),
        ]
        + [rand_tile(j, 0) for j in range(R)]
        + [rand_tile(j, groups) for j in range(R)]
    )
    rand_spec = pl.BlockSpec((1, R * BS, cw), lambda n, h, s: (n, 0, h))
    prob_spec = pl.BlockSpec((1, HG, BS, g), lambda n, h, s: (n, h, 0, 0))
    out_specs = [row_spec, row_spec, rand_spec, rand_spec, prob_spec, prob_spec]
    out_shape = [
        jax.ShapeDtypeStruct((rows, width), jnp.bfloat16),
        jax.ShapeDtypeStruct((rows, width), jnp.bfloat16),
        jax.ShapeDtypeStruct((nbd, R * BS, width), jnp.bfloat16),
        jax.ShapeDtypeStruct((nbd, R * BS, width), jnp.bfloat16),
        jax.ShapeDtypeStruct((nbd, heads, BS, g), jnp.bfloat16),
        jax.ShapeDtypeStruct((nbd, heads, BS, g), jnp.bfloat16),
    ]
    grid_spec = pltpu.PrefetchScalarGridSpec(
        num_scalar_prefetch=1,
        grid=(nbd, groups),
        in_specs=in_specs,
        out_specs=out_specs,
    )
    args = [query, dout, mask] + [padded] * 6 + [glob] * 2 + [fetched] * (2 * R)
    out, dq, rk, rv, pb, dsb = pl.pallas_call(
        scores_kernel,
        grid_spec=grid_spec,
        out_shape=out_shape,
        interpret=INTERPRET,
    )(slots, *args)

    row2 = pl.BlockSpec((BS, cw), lambda n, h: (n, h))
    prob2 = pl.BlockSpec((1, HG, BS, g), lambda n, h: (n, h, 0, 0))

    def term_spec(size):
        return pl.BlockSpec((1, size, cw), lambda n, h: (n, 0, h))

    wk, wv, gk, gv = pl.pallas_call(
        terms_kernel,
        grid=(nbd, groups),
        in_specs=[row2, row2, prob2, prob2],
        out_specs=[term_spec(3 * BS), term_spec(3 * BS), term_spec(2 * BS), term_spec(2 * BS)],
        out_shape=[
            jax.ShapeDtypeStruct((nbd, 3 * BS, width), jnp.float32),
            jax.ShapeDtypeStruct((nbd, 3 * BS, width), jnp.float32),
            jax.ShapeDtypeStruct((nbd, 2 * BS, width), jnp.float32),
            jax.ShapeDtypeStruct((nbd, 2 * BS, width), jnp.float32),
        ],
        interpret=INTERPRET,
    )(query, dout, pb, dsb)
    return out, dq, wk, wv, gk, gv, rk, rv


def overlap(terms, nbd):
    width = terms.shape[-1]
    w4 = terms.reshape(nbd, 3, BS, width)
    return (
        jnp.pad(w4[:, 0], ((0, 2), (0, 0), (0, 0)))
        + jnp.pad(w4[:, 1], ((1, 1), (0, 0), (0, 0)))
        + jnp.pad(w4[:, 2], ((2, 0), (0, 0), (0, 0)))
    )


def body(query, key, value, dout, rand):
    rows, width = query.shape
    ndev = lax.axis_size(("head", "blk"))
    me = lax.axis_index(("head", "blk"))
    nbd = rows // BS
    total = nbd * ndev
    cap = (R * nbd + ndev - 1) // ndev
    pf = jnp.float32
    span = (5 + R) * BS
    pair = jnp.concatenate([key, value], axis=1)
    padded = extended(pair, ((("head", "blk"), 0),), BS)
    glob = from_root(pair[: 2 * BS], ("head", "blk"))
    flat = rand.reshape(ndev, nbd * R)
    owner = flat // nbd
    local = flat - owner * nbd
    hit = owner == me
    order = jnp.cumsum(hit.astype(jnp.int32), axis=1) - 1
    slot_ids = jnp.arange(cap, dtype=jnp.int32)
    chosen = hit[:, None, :] & (order[:, None, :] == slot_ids[None, :, None])
    block_id = jnp.sum(jnp.where(chosen, local[:, None, :], 0), axis=2).reshape(-1)
    filled = jnp.any(chosen, axis=2).reshape(-1)
    tiles = pair.reshape(nbd, BS, 2 * width)
    outgoing = jnp.take(
        tiles, jnp.where(filled, block_id, nbd), axis=0, mode="fill", fill_value=0
    )
    fetched = lax.all_to_all(outgoing, ("head", "blk"), split_axis=0, concat_axis=0, tiled=True)
    mine = lax.dynamic_slice_in_dim(rand, me * nbd, nbd, 0).reshape(-1)
    mine_owner = mine // nbd
    count = mine.shape[0]
    earlier = jnp.arange(count)[:, None] > jnp.arange(count)[None, :]
    same = mine_owner[:, None] == mine_owner[None, :]
    mine_rank = jnp.sum(earlier & same, axis=1)
    mine_slot = (mine_owner * cap + mine_rank).astype(jnp.int32)
    first = me * nbd + jnp.arange(nbd, dtype=jnp.int32)
    always = first >= 0
    valid = jnp.concatenate(
        [
            jnp.stack([first > 0, always, first < total - 1, always, always], axis=1),
            jnp.ones((nbd, R), bool),
        ],
        axis=1,
    )
    mask = jnp.repeat(valid, BS, axis=1).astype(pf).reshape(nbd, 1, span)
    out, dq, wk, wv, gk, gv, rk, rv = attention(query, dout, mask, padded, glob, fetched, mine_slot)
    sk = overlap(wk, nbd)
    sv = overlap(wv, nbd)
    rims = jnp.concatenate(
        [
            jnp.concatenate([sk[0], sv[0]], axis=-1),
            jnp.concatenate([sk[nbd + 1], sv[nbd + 1]], axis=-1),
        ],
        axis=0,
    )
    arrived = extended(rims.astype(jnp.bfloat16), ((("head", "blk"), 0),), BS).astype(pf)
    own = jnp.concatenate([sk[1 : nbd + 1], sv[1 : nbd + 1]], axis=-1)
    glob_grad = jnp.concatenate([jnp.sum(gk, axis=0), jnp.sum(gv, axis=0)], axis=-1).reshape(
        2, BS, 2 * width
    )
    glob_total = lax.psum(glob_grad.astype(jnp.bfloat16), ("head", "blk")).astype(pf)
    edge = jnp.concatenate(
        [arrived[None, :BS], jnp.zeros((nbd - 2, BS, 2 * width), pf), arrived[None, 3 * BS :]], axis=0
    )
    lead = jnp.pad(jnp.where(me == 0, glob_total, 0.0), ((0, nbd - 2), (0, 0), (0, 0)))
    own = own + edge + lead
    rand_grad = jnp.concatenate([rk, rv], axis=-1).reshape(nbd * R, BS, 2 * width)
    match = mine_slot[None, :] == jnp.arange(ndev * cap, dtype=jnp.int32)[:, None]
    source = jnp.argmax(match, axis=1)
    returning = jnp.take(
        rand_grad,
        jnp.where(jnp.any(match, axis=1), source, nbd * R),
        axis=0,
        mode="fill",
        fill_value=0,
    )
    back = lax.all_to_all(returning, ("head", "blk"), split_axis=0, concat_axis=0, tiled=True)
    onehot = (
        (block_id[None, :] == jnp.arange(nbd, dtype=jnp.int32)[:, None]) & filled[None, :]
    ).astype(jnp.bfloat16)
    own = own + jnp.dot(
        onehot, back.reshape(ndev * cap, BS * 2 * width), preferred_element_type=pf
    ).reshape(nbd, BS, 2 * width)
    dk = own[..., :width].astype(jnp.bfloat16).reshape(rows, width)
    dv = own[..., width:].astype(jnp.bfloat16).reshape(rows, width)
    return (out, dq, dk, dv)


def solution(mesh):
    placed = (
        P(("dp", "head", "blk"), None),
        P(("dp", "head", "blk"), None),
        P(("dp", "head", "blk"), None),
        P(("dp", "head", "blk"), None),
        P("dp", None),
    )
    return jax.shard_map(
        body,
        mesh=mesh,
        in_specs=placed,
        out_specs=(
            P(("dp", "head", "blk"), None),
            P(("dp", "head", "blk"), None),
            P(("dp", "head", "blk"), None),
            P(("dp", "head", "blk"), None),
        ),
        check_vma=False,
    )
```

```python
import math

import jax
import jax.numpy as jnp
from jax import lax
from jax.experimental import pallas as pl
from jax.experimental.pallas import tpu as pltpu
from jax.sharding import PartitionSpec as P

HD = 128
BS = 64
R = 3


NEG = -1e30
INTERPRET = False
HG = 8


def extended(block, sides, width):
    for axis, dim in sides:
        count = lax.axis_size(axis)
        forward = [(i, i + 1) for i in range(count - 1)]
        backward = [(target, source) for source, target in forward]
        low = lax.ppermute(
            lax.slice_in_dim(block, block.shape[dim] - width, None, axis=dim), axis, forward
        )
        high = lax.ppermute(lax.slice_in_dim(block, 0, width, axis=dim), axis, backward)
        block = jnp.concatenate([low, block, high], axis=dim)
    return block


def from_root(value, axis, source):
    kept = jnp.where(lax.axis_index(axis) == source, value, 0).astype(value.dtype)
    return lax.psum(kept, axis)


def scores_kernel(
    slots_ref, q_ref, do_ref, mask_ref,
    kw0, kw1, kw2, vw0, vw1, vw2, kg, vg, kr0, kr1, kr2, vr0, vr1, vr2,
    out_ref, dq_ref, rk_ref, rv_ref, pb_ref, dsb_ref,
):
    pf = jnp.float32
    scale = 1.0 / math.sqrt(HD)
    nt = (((1,), (1,)), ((), ()))
    tn = (((0,), (0,)), ((), ()))
    g = 5 * BS
    valid = mask_ref[0] > 0
    for t in range(HG):
        c = slice(t * HD, (t + 1) * HD)
        q = q_ref[:, c]
        do = do_ref[:, c]
        k = jnp.concatenate(
            [kw0[:, c], kw1[:, c], kw2[:, c], kg[:, c], kr0[0, :, c], kr1[0, :, c], kr2[0, :, c]], axis=0
        )
        v = jnp.concatenate(
            [vw0[:, c], vw1[:, c], vw2[:, c], vg[:, c], vr0[0, :, c], vr1[0, :, c], vr2[0, :, c]], axis=0
        )
        s = lax.dot_general(q, k, nt, preferred_element_type=pf) * scale
        s = jnp.where(valid, s, NEG)
        top = jnp.max(s, axis=1, keepdims=True)
        e = jnp.exp(s - top)
        p = e / jnp.sum(e, axis=1, keepdims=True)
        pb = p.astype(jnp.bfloat16)
        ob = jnp.dot(pb, v, preferred_element_type=pf).astype(jnp.bfloat16)
        out_ref[:, c] = ob
        delta = jnp.sum(do.astype(pf) * ob.astype(pf), axis=1, keepdims=True)
        dp = lax.dot_general(do, v, nt, preferred_element_type=pf)
        ds = p * (dp - delta)
        dsb = ds.astype(jnp.bfloat16)
        dq_ref[:, c] = (jnp.dot(dsb, k, preferred_element_type=pf) * scale).astype(jnp.bfloat16)
        rk_ref[0, :, c] = (
            lax.dot_general(dsb[:, g:], q, tn, preferred_element_type=pf) * scale
        ).astype(jnp.bfloat16)
        rv_ref[0, :, c] = lax.dot_general(pb[:, g:], do, tn, preferred_element_type=pf).astype(jnp.bfloat16)
        pb_ref[0, t] = pb[:, :g]
        dsb_ref[0, t] = dsb[:, :g]


def terms_kernel(q_ref, do_ref, pb_ref, dsb_ref, wk_ref, wv_ref, gk_ref, gv_ref):
    pf = jnp.float32
    scale = 1.0 / math.sqrt(HD)
    tn = (((0,), (0,)), ((), ()))
    w = 3 * BS
    for t in range(HG):
        c = slice(t * HD, (t + 1) * HD)
        kt = lax.dot_general(dsb_ref[0, t], q_ref[:, c], tn, preferred_element_type=pf) * scale
        vt = lax.dot_general(pb_ref[0, t], do_ref[:, c], tn, preferred_element_type=pf)
        wk_ref[0, :, c] = kt[:w]
        wv_ref[0, :, c] = vt[:w]
        gk_ref[0, :, c] = kt[w:]
        gv_ref[0, :, c] = vt[w:]


def attention(query, dout, mask, padded, glob, fetched, slots):
    rows, width = query.shape
    heads = width // HD
    groups = heads // HG
    cw = HG * HD
    nbd = rows // BS
    span = (5 + R) * BS
    g = 5 * BS

    def tile(j, col):
        return pl.BlockSpec((BS, cw), lambda n, h, s: (n + j, h + col))

    def rand_tile(j, col):
        return pl.BlockSpec((1, BS, cw), lambda n, h, s: (s[n * R + j], 0, h + col))

    row_spec = pl.BlockSpec((BS, cw), lambda n, h, s: (n, h))
    in_specs = (
        [row_spec, row_spec, pl.BlockSpec((1, 1, span), lambda n, h, s: (n, 0, 0))]
        + [tile(j, 0) for j in range(3)]
        + [tile(j, groups) for j in range(3)]
        + [
            pl.BlockSpec((2 * BS, cw), lambda n, h, s: (0, h)),
            pl.BlockSpec((2 * BS, cw), lambda n, h, s: (0, h + groups)),
        ]
        + [rand_tile(j, 0) for j in range(R)]
        + [rand_tile(j, groups) for j in range(R)]
    )
    rand_spec = pl.BlockSpec((1, R * BS, cw), lambda n, h, s: (n, 0, h))
    prob_spec = pl.BlockSpec((1, HG, BS, g), lambda n, h, s: (n, h, 0, 0))
    out_specs = [row_spec, row_spec, rand_spec, rand_spec, prob_spec, prob_spec]
    out_shape = [
        jax.ShapeDtypeStruct((rows, width), jnp.bfloat16),
        jax.ShapeDtypeStruct((rows, width), jnp.bfloat16),
        jax.ShapeDtypeStruct((nbd, R * BS, width), jnp.bfloat16),
        jax.ShapeDtypeStruct((nbd, R * BS, width), jnp.bfloat16),
        jax.ShapeDtypeStruct((nbd, heads, BS, g), jnp.bfloat16),
        jax.ShapeDtypeStruct((nbd, heads, BS, g), jnp.bfloat16),
    ]
    grid_spec = pltpu.PrefetchScalarGridSpec(
        num_scalar_prefetch=1,
        grid=(nbd, groups),
        in_specs=in_specs,
        out_specs=out_specs,
    )
    args = [query, dout, mask] + [padded] * 6 + [glob] * 2 + [fetched] * (2 * R)
    out, dq, rk, rv, pb, dsb = pl.pallas_call(
        scores_kernel,
        grid_spec=grid_spec,
        out_shape=out_shape,
        interpret=INTERPRET,
    )(slots, *args)

    row2 = pl.BlockSpec((BS, cw), lambda n, h: (n, h))
    prob2 = pl.BlockSpec((1, HG, BS, g), lambda n, h: (n, h, 0, 0))

    def term_spec(size):
        return pl.BlockSpec((1, size, cw), lambda n, h: (n, 0, h))

    wk, wv, gk, gv = pl.pallas_call(
        terms_kernel,
        grid=(nbd, groups),
        in_specs=[row2, row2, prob2, prob2],
        out_specs=[term_spec(3 * BS), term_spec(3 * BS), term_spec(2 * BS), term_spec(2 * BS)],
        out_shape=[
            jax.ShapeDtypeStruct((nbd, 3 * BS, width), jnp.float32),
            jax.ShapeDtypeStruct((nbd, 3 * BS, width), jnp.float32),
            jax.ShapeDtypeStruct((nbd, 2 * BS, width), jnp.float32),
            jax.ShapeDtypeStruct((nbd, 2 * BS, width), jnp.float32),
        ],
        interpret=INTERPRET,
    )(query, dout, pb, dsb)
    return out, dq, wk, wv, gk, gv, rk, rv


def overlap(terms, nbd):
    width = terms.shape[-1]
    w4 = terms.reshape(nbd, 3, BS, width)
    return (
        jnp.pad(w4[:, 0], ((0, 2), (0, 0), (0, 0)))
        + jnp.pad(w4[:, 1], ((1, 1), (0, 0), (0, 0)))
        + jnp.pad(w4[:, 2], ((2, 0), (0, 0), (0, 0)))
    )


def body(query, key, value, dout, rand):
    rows, width = query.shape
    ndev = lax.axis_size(("head", "blk"))
    me = lax.axis_index(("head", "blk"))
    nbd = rows // BS
    total = nbd * ndev
    cap = (R * nbd + ndev - 1) // ndev
    pf = jnp.float32
    span = (5 + R) * BS
    pair = jnp.concatenate([key, value], axis=1)
    padded = extended(pair, ((("head", "blk"), 0),), BS)
    glob = from_root(pair[: 2 * BS], ("head", "blk"), 0)
    flat = rand.reshape(ndev, nbd * R)
    owner = flat // nbd
    local = flat - owner * nbd
    hit = owner == me
    order = jnp.cumsum(hit.astype(jnp.int32), axis=1) - 1
    slot_ids = jnp.arange(cap, dtype=jnp.int32)
    chosen = hit[:, None, :] & (order[:, None, :] == slot_ids[None, :, None])
    block_id = jnp.sum(jnp.where(chosen, local[:, None, :], 0), axis=2).reshape(-1)
    filled = jnp.any(chosen, axis=2).reshape(-1)
    tiles = pair.reshape(nbd, BS, 2 * width)
    outgoing = jnp.where(
        filled[:, None, None], jnp.take(tiles, block_id, axis=0), jnp.zeros((), pair.dtype)
    )
    fetched = lax.all_to_all(outgoing, ("head", "blk"), split_axis=0, concat_axis=0, tiled=True)
    mine = lax.dynamic_slice_in_dim(rand, me * nbd, nbd, 0).reshape(-1)
    mine_owner = mine // nbd
    count = mine.shape[0]
    earlier = jnp.arange(count)[:, None] > jnp.arange(count)[None, :]
    same = mine_owner[:, None] == mine_owner[None, :]
    mine_rank = jnp.sum(earlier & same, axis=1)
    mine_slot = (mine_owner * cap + mine_rank).astype(jnp.int32)
    first = me * nbd + jnp.arange(nbd, dtype=jnp.int32)
    always = first >= 0
    valid = jnp.concatenate(
        [
            jnp.stack([first > 0, always, first < total - 1, always, always], axis=1),
            jnp.ones((nbd, R), bool),
        ],
        axis=1,
    )
    mask = jnp.repeat(valid, BS, axis=1).astype(pf).reshape(nbd, 1, span)
    out, dq, wk, wv, gk, gv, rk, rv = attention(query, dout, mask, padded, glob, fetched, mine_slot)
    sk = overlap(wk, nbd)
    sv = overlap(wv, nbd)
    rims = jnp.concatenate(
        [
            jnp.concatenate([sk[0], sv[0]], axis=-1),
            jnp.concatenate([sk[nbd + 1], sv[nbd + 1]], axis=-1),
        ],
        axis=0,
    )
    arrived = extended(rims.astype(jnp.bfloat16), ((("head", "blk"), 0),), BS).astype(pf)
    own = jnp.concatenate([sk[1 : nbd + 1], sv[1 : nbd + 1]], axis=-1)
    glob_grad = jnp.concatenate([jnp.sum(gk, axis=0), jnp.sum(gv, axis=0)], axis=-1).reshape(
        2, BS, 2 * width
    )
    glob_total = lax.psum(glob_grad.astype(jnp.bfloat16), ("head", "blk")).astype(pf)
    edge = jnp.concatenate(
        [arrived[None, :BS], jnp.zeros((nbd - 2, BS, 2 * width), pf), arrived[None, 3 * BS :]], axis=0
    )
    lead = jnp.pad(jnp.where(me == 0, glob_total, 0.0), ((0, nbd - 2), (0, 0), (0, 0)))
    own = own + edge + lead
    rand_grad = jnp.concatenate([rk, rv], axis=-1).reshape(nbd * R, BS, 2 * width)
    match = mine_slot[None, :] == jnp.arange(ndev * cap, dtype=jnp.int32)[:, None]
    source = jnp.argmax(match, axis=1)
    returning = jnp.where(
        jnp.any(match, axis=1)[:, None, None],
        jnp.take(rand_grad, source, axis=0),
        jnp.zeros((), jnp.bfloat16),
    )
    back = lax.all_to_all(returning, ("head", "blk"), split_axis=0, concat_axis=0, tiled=True)
    onehot = (
        (block_id[None, :] == jnp.arange(nbd, dtype=jnp.int32)[:, None]) & filled[None, :]
    ).astype(jnp.bfloat16)
    own = own + jnp.dot(
        onehot, back.reshape(ndev * cap, BS * 2 * width), preferred_element_type=pf
    ).reshape(nbd, BS, 2 * width)
    dk = own[..., :width].astype(jnp.bfloat16).reshape(rows, width)
    dv = own[..., width:].astype(jnp.bfloat16).reshape(rows, width)
    return (out, dq, dk, dv)


def solution(mesh):
    placed = (
        P(("dp", "head", "blk"), None),
        P(("dp", "head", "blk"), None),
        P(("dp", "head", "blk"), None),
        P(("dp", "head", "blk"), None),
        P("dp", None),
    )
    return jax.shard_map(
        body,
        mesh=mesh,
        in_specs=placed,
        out_specs=(
            P(("dp", "head", "blk"), None),
            P(("dp", "head", "blk"), None),
            P(("dp", "head", "blk"), None),
            P(("dp", "head", "blk"), None),
        ),
        check_vma=False,
    )
```

```python
import math

import jax
import jax.numpy as jnp
from jax import lax
from jax.experimental import pallas as pl
from jax.experimental.pallas import tpu as pltpu
from jax.sharding import PartitionSpec as P

HD = 128
BS = 64
R = 3


NEG = -1e30
INTERPRET = False
HG = 16


def extended(block, sides, width):
    for axis, dim in sides:
        count = lax.axis_size(axis)
        forward = [(i, i + 1) for i in range(count - 1)]
        backward = [(target, source) for source, target in forward]
        low = lax.ppermute(
            lax.slice_in_dim(block, block.shape[dim] - width, None, axis=dim), axis, forward
        )
        high = lax.ppermute(lax.slice_in_dim(block, 0, width, axis=dim), axis, backward)
        block = jnp.concatenate([low, block, high], axis=dim)
    return block


def from_root(value, axis, source):
    kept = jnp.where(lax.axis_index(axis) == source, value, 0).astype(value.dtype)
    return lax.psum(kept, axis)


def scores_kernel(
    slots_ref, q_ref, do_ref, mask_ref,
    kw0, kw1, kw2, vw0, vw1, vw2, kg, vg, kr0, kr1, kr2, vr0, vr1, vr2,
    out_ref, dq_ref, rk_ref, rv_ref, pb_ref, dsb_ref,
):
    pf = jnp.float32
    scale = 1.0 / math.sqrt(HD)
    nt = (((1,), (1,)), ((), ()))
    tn = (((0,), (0,)), ((), ()))
    g = 5 * BS
    valid = mask_ref[0] > 0
    for t in range(HG):
        c = slice(t * HD, (t + 1) * HD)
        q = q_ref[:, c]
        do = do_ref[:, c]
        k = jnp.concatenate(
            [kw0[:, c], kw1[:, c], kw2[:, c], kg[:, c], kr0[0, :, c], kr1[0, :, c], kr2[0, :, c]], axis=0
        )
        v = jnp.concatenate(
            [vw0[:, c], vw1[:, c], vw2[:, c], vg[:, c], vr0[0, :, c], vr1[0, :, c], vr2[0, :, c]], axis=0
        )
        s = lax.dot_general(q, k, nt, preferred_element_type=pf) * scale
        s = jnp.where(valid, s, NEG)
        top = jnp.max(s, axis=1, keepdims=True)
        e = jnp.exp(s - top)
        p = e / jnp.sum(e, axis=1, keepdims=True)
        pb = p.astype(jnp.bfloat16)
        ob = jnp.dot(pb, v, preferred_element_type=pf).astype(jnp.bfloat16)
        out_ref[:, c] = ob
        delta = jnp.sum(do.astype(pf) * ob.astype(pf), axis=1, keepdims=True)
        dp = lax.dot_general(do, v, nt, preferred_element_type=pf)
        ds = p * (dp - delta)
        dsb = ds.astype(jnp.bfloat16)
        dq_ref[:, c] = (jnp.dot(dsb, k, preferred_element_type=pf) * scale).astype(jnp.bfloat16)
        rk_ref[0, :, c] = (
            lax.dot_general(dsb[:, g:], q, tn, preferred_element_type=pf) * scale
        ).astype(jnp.bfloat16)
        rv_ref[0, :, c] = lax.dot_general(pb[:, g:], do, tn, preferred_element_type=pf).astype(jnp.bfloat16)
        pb_ref[0, t] = pb[:, :g]
        dsb_ref[0, t] = dsb[:, :g]


def terms_kernel(q_ref, do_ref, pb_ref, dsb_ref, wk_ref, wv_ref, gk_ref, gv_ref):
    pf = jnp.float32
    scale = 1.0 / math.sqrt(HD)
    tn = (((0,), (0,)), ((), ()))
    w = 3 * BS
    for t in range(HG):
        c = slice(t * HD, (t + 1) * HD)
        kt = lax.dot_general(dsb_ref[0, t], q_ref[:, c], tn, preferred_element_type=pf) * scale
        vt = lax.dot_general(pb_ref[0, t], do_ref[:, c], tn, preferred_element_type=pf)
        wk_ref[0, :, c] = kt[:w]
        wv_ref[0, :, c] = vt[:w]
        gk_ref[0, :, c] = kt[w:]
        gv_ref[0, :, c] = vt[w:]


def attention(query, dout, mask, padded, glob, fetched, slots):
    rows, width = query.shape
    heads = width // HD
    groups = heads // HG
    cw = HG * HD
    nbd = rows // BS
    span = (5 + R) * BS
    g = 5 * BS

    def tile(j, col):
        return pl.BlockSpec((BS, cw), lambda n, h, s: (n + j, h + col))

    def rand_tile(j, col):
        return pl.BlockSpec((1, BS, cw), lambda n, h, s: (s[n * R + j], 0, h + col))

    row_spec = pl.BlockSpec((BS, cw), lambda n, h, s: (n, h))
    in_specs = (
        [row_spec, row_spec, pl.BlockSpec((1, 1, span), lambda n, h, s: (n, 0, 0))]
        + [tile(j, 0) for j in range(3)]
        + [tile(j, groups) for j in range(3)]
        + [
            pl.BlockSpec((2 * BS, cw), lambda n, h, s: (0, h)),
            pl.BlockSpec((2 * BS, cw), lambda n, h, s: (0, h + groups)),
        ]
        + [rand_tile(j, 0) for j in range(R)]
        + [rand_tile(j, groups) for j in range(R)]
    )
    rand_spec = pl.BlockSpec((1, R * BS, cw), lambda n, h, s: (n, 0, h))
    prob_spec = pl.BlockSpec((1, HG, BS, g), lambda n, h, s: (n, h, 0, 0))
    out_specs = [row_spec, row_spec, rand_spec, rand_spec, prob_spec, prob_spec]
    out_shape = [
        jax.ShapeDtypeStruct((rows, width), jnp.bfloat16),
        jax.ShapeDtypeStruct((rows, width), jnp.bfloat16),
        jax.ShapeDtypeStruct((nbd, R * BS, width), jnp.bfloat16),
        jax.ShapeDtypeStruct((nbd, R * BS, width), jnp.bfloat16),
        jax.ShapeDtypeStruct((nbd, heads, BS, g), jnp.bfloat16),
        jax.ShapeDtypeStruct((nbd, heads, BS, g), jnp.bfloat16),
    ]
    grid_spec = pltpu.PrefetchScalarGridSpec(
        num_scalar_prefetch=1,
        grid=(nbd, groups),
        in_specs=in_specs,
        out_specs=out_specs,
    )
    args = [query, dout, mask] + [padded] * 6 + [glob] * 2 + [fetched] * (2 * R)
    out, dq, rk, rv, pb, dsb = pl.pallas_call(
        scores_kernel,
        grid_spec=grid_spec,
        out_shape=out_shape,
        interpret=INTERPRET,
    )(slots, *args)

    row2 = pl.BlockSpec((BS, cw), lambda n, h: (n, h))
    prob2 = pl.BlockSpec((1, HG, BS, g), lambda n, h: (n, h, 0, 0))

    def term_spec(size):
        return pl.BlockSpec((1, size, cw), lambda n, h: (n, 0, h))

    wk, wv, gk, gv = pl.pallas_call(
        terms_kernel,
        grid=(nbd, groups),
        in_specs=[row2, row2, prob2, prob2],
        out_specs=[term_spec(3 * BS), term_spec(3 * BS), term_spec(2 * BS), term_spec(2 * BS)],
        out_shape=[
            jax.ShapeDtypeStruct((nbd, 3 * BS, width), jnp.float32),
            jax.ShapeDtypeStruct((nbd, 3 * BS, width), jnp.float32),
            jax.ShapeDtypeStruct((nbd, 2 * BS, width), jnp.float32),
            jax.ShapeDtypeStruct((nbd, 2 * BS, width), jnp.float32),
        ],
        interpret=INTERPRET,
    )(query, dout, pb, dsb)
    return out, dq, wk, wv, gk, gv, rk, rv


def overlap(terms, nbd):
    width = terms.shape[-1]
    w4 = terms.reshape(nbd, 3, BS, width)
    return (
        jnp.pad(w4[:, 0], ((0, 2), (0, 0), (0, 0)))
        + jnp.pad(w4[:, 1], ((1, 1), (0, 0), (0, 0)))
        + jnp.pad(w4[:, 2], ((2, 0), (0, 0), (0, 0)))
    )


def body(query, key, value, dout, rand):
    rows, width = query.shape
    ndev = lax.axis_size(("head", "blk"))
    me = lax.axis_index(("head", "blk"))
    nbd = rows // BS
    total = nbd * ndev
    cap = (R * nbd + ndev - 1) // ndev
    pf = jnp.float32
    span = (5 + R) * BS
    pair = jnp.concatenate([key, value], axis=1)
    padded = extended(pair, ((("head", "blk"), 0),), BS)
    glob = from_root(pair[: 2 * BS], ("head", "blk"), 0)
    flat = rand.reshape(ndev, nbd * R)
    owner = flat // nbd
    local = flat - owner * nbd
    hit = owner == me
    order = jnp.cumsum(hit.astype(jnp.int32), axis=1) - 1
    slot_ids = jnp.arange(cap, dtype=jnp.int32)
    chosen = hit[:, None, :] & (order[:, None, :] == slot_ids[None, :, None])
    block_id = jnp.sum(jnp.where(chosen, local[:, None, :], 0), axis=2).reshape(-1)
    filled = jnp.any(chosen, axis=2).reshape(-1)
    tiles = pair.reshape(nbd, BS, 2 * width)
    outgoing = jnp.where(
        filled[:, None, None], jnp.take(tiles, block_id, axis=0), jnp.zeros((), pair.dtype)
    )
    fetched = lax.all_to_all(outgoing, ("head", "blk"), split_axis=0, concat_axis=0, tiled=True)
    mine = lax.dynamic_slice_in_dim(rand, me * nbd, nbd, 0).reshape(-1)
    mine_owner = mine // nbd
    count = mine.shape[0]
    earlier = jnp.arange(count)[:, None] > jnp.arange(count)[None, :]
    same = mine_owner[:, None] == mine_owner[None, :]
    mine_rank = jnp.sum(earlier & same, axis=1)
    mine_slot = (mine_owner * cap + mine_rank).astype(jnp.int32)
    first = me * nbd + jnp.arange(nbd, dtype=jnp.int32)
    always = first >= 0
    valid = jnp.concatenate(
        [
            jnp.stack([first > 0, always, first < total - 1, always, always], axis=1),
            jnp.ones((nbd, R), bool),
        ],
        axis=1,
    )
    mask = jnp.repeat(valid, BS, axis=1).astype(pf).reshape(nbd, 1, span)
    out, dq, wk, wv, gk, gv, rk, rv = attention(query, dout, mask, padded, glob, fetched, mine_slot)
    sk = overlap(wk, nbd)
    sv = overlap(wv, nbd)
    rims = jnp.concatenate(
        [
            jnp.concatenate([sk[0], sv[0]], axis=-1),
            jnp.concatenate([sk[nbd + 1], sv[nbd + 1]], axis=-1),
        ],
        axis=0,
    )
    arrived = extended(rims.astype(jnp.bfloat16), ((("head", "blk"), 0),), BS).astype(pf)
    own = jnp.concatenate([sk[1 : nbd + 1], sv[1 : nbd + 1]], axis=-1)
    glob_grad = jnp.concatenate([jnp.sum(gk, axis=0), jnp.sum(gv, axis=0)], axis=-1).reshape(
        2, BS, 2 * width
    )
    glob_total = lax.psum(glob_grad.astype(jnp.bfloat16), ("head", "blk")).astype(pf)
    edge = jnp.concatenate(
        [arrived[None, :BS], jnp.zeros((nbd - 2, BS, 2 * width), pf), arrived[None, 3 * BS :]], axis=0
    )
    lead = jnp.pad(jnp.where(me == 0, glob_total, 0.0), ((0, nbd - 2), (0, 0), (0, 0)))
    own = own + edge + lead
    rand_grad = jnp.concatenate([rk, rv], axis=-1).reshape(nbd * R, BS, 2 * width)
    match = mine_slot[None, :] == jnp.arange(ndev * cap, dtype=jnp.int32)[:, None]
    source = jnp.argmax(match, axis=1)
    returning = jnp.where(
        jnp.any(match, axis=1)[:, None, None],
        jnp.take(rand_grad, source, axis=0),
        jnp.zeros((), jnp.bfloat16),
    )
    back = lax.all_to_all(returning, ("head", "blk"), split_axis=0, concat_axis=0, tiled=True)
    onehot = (
        (block_id[None, :] == jnp.arange(nbd, dtype=jnp.int32)[:, None]) & filled[None, :]
    ).astype(jnp.bfloat16)
    own = own + jnp.dot(
        onehot, back.reshape(ndev * cap, BS * 2 * width), preferred_element_type=pf
    ).reshape(nbd, BS, 2 * width)
    dk = own[..., :width].astype(jnp.bfloat16).reshape(rows, width)
    dv = own[..., width:].astype(jnp.bfloat16).reshape(rows, width)
    return (out, dq, dk, dv)


def solution(mesh):
    placed = (
        P(("dp", "head", "blk"), None),
        P(("dp", "head", "blk"), None),
        P(("dp", "head", "blk"), None),
        P(("dp", "head", "blk"), None),
        P("dp", None),
    )
    return jax.shard_map(
        body,
        mesh=mesh,
        in_specs=placed,
        out_specs=(
            P(("dp", "head", "blk"), None),
            P(("dp", "head", "blk"), None),
            P(("dp", "head", "blk"), None),
            P(("dp", "head", "blk"), None),
        ),
        check_vma=False,
    )
```
